256 devices in a mesh: req: 16 (over x, y), cuts: 16 (over z, core).
Axes of the slice: x: 4, y: 4, z: 8, core: 2. Of those that a mesh axis runs over, the one named last changes fastest.
Arguments:
- queries: bfloat16 [16, 2048, 1024], P('req', 'cuts')
- new_keys: bfloat16 [16, 2048, 1024], P('req', 'cuts'), may hold values from -6 to 6
- new_values: bfloat16 [16, 2048, 1024], P('req', 'cuts'), may hold values from -12 to 12
- cache_keys: bfloat16 [16, 4096, 1024], P('req', 'cuts')
- cache_values: bfloat16 [16, 4096, 1024], P('req', 'cuts'), may hold values from -12 to 12
- cache_lengths: int32 [16], P('req'), may hold values from 2 to 4096, as said below
- relative_bias: float32 [16, 32], replicated, may hold values from -4 to 4
- residual: bfloat16 [16, 2048, 1024], P('req', 'cuts')
- out_weight: bfloat16 [1024, 1024], replicated, may hold values from -0.1875 to 0.1875
- norm_gain: bfloat16 [1024], replicated, may hold values from 0.5 to 1.5
- router_weight: bfloat16 [1024, 16], replicated, may hold values from -0.1875 to 0.1875
- routes: int32 [16, 2048, 2], P('req', 'cuts'), may hold values from 0 to 15, all different within a row; in each aligned block of 128 rows (0 to 127, 128 to 255, ..., all dimensions but the last counted through in order) at most 20 rows name the same one
- gate_weight: bfloat16 [16, 1024, 2816], P('req', None, 'cuts'), may hold values from -0.1875 to 0.1875
- up_weight: bfloat16 [16, 1024, 2816], P('req', None, 'cuts'), may hold values from -0.1875 to 0.1875
- down_weight: bfloat16 [16, 1024, 2816], P('req', None, 'cuts'), may hold values from -0.109375 to 0.109375
Outputs:
- layer_out: bfloat16 [16, 2048, 1024], P('req', 'cuts')
The draws below stay inside these ranges and needn't reach their ends.
Inputs may be any that keep to these rules, and one draw needn't show every extreme that they name: `cache_lengths`: each cached length lies under 256 or above 3840; some request's cache is full. `routes`: among the 128 tokens of one device no expert is named by more than 20 tokens, a bound that some block reaches.
All inputs are finite; a program needn't handle non-finite values.
Results may differ from the reference program's by a relative error of at most 0.03.
Values may be sent and summed in bfloat16 or wider, within the bound.
No kernel may reach another device: no remote copies, remote signals or barrier semaphores. Data moves between devices by JAX's collectives and lax.ppermute only.
A program may use at most 128 MiB of HBM per device.

```python
import math
import jax
import jax.numpy as jnp
import numpy as np
from jax import lax

D = 1024
H = 16
HD = 64
FF = 2816
TOP = 2
BUCKETS = 32
MAXDIST = 128
Q_DEV = 128
CACHE_DEV = 256
REQS = 16
EXPERTS = 16
STRETCH = 2048
CACHE = 4096
CAP = 20
SHORT = 256
N_CUTS = 16


def draw_queries(key, part):
    values = jax.random.normal(jax.random.fold_in(key, 21), (REQS, STRETCH, D), jnp.float32)
    return values.astype(jnp.bfloat16)


def draw_cache_keys(key, part):
    values = jax.random.normal(jax.random.fold_in(key, 31), (REQS, CACHE, D), jnp.float32)
    return values.astype(jnp.bfloat16)


def draw_residual(key, part):
    spread = jax.random.uniform(jax.random.fold_in(key, 41), (REQS, STRETCH, 1), jnp.float32)
    row_scale = 0.02 * jnp.exp(spread * math.log(10.0))
    values = jax.random.normal(jax.random.fold_in(key, 42), (REQS, STRETCH, D), jnp.float32)
    return (values * row_scale).astype(jnp.bfloat16)


def draw_cache_lengths(key, part):
    long_flag = jax.random.randint(jax.random.fold_in(key, 51), (REQS,), 0, 2)
    short_length = jax.random.randint(jax.random.fold_in(key, 52), (REQS,), 2, SHORT)
    long_length = jax.random.randint(jax.random.fold_in(key, 53), (REQS,), CACHE - CACHE_DEV + 1, CACHE + 1)
    full_request = jax.random.randint(jax.random.fold_in(key, 54), (), 0, REQS)
    lengths = jnp.where(long_flag == 1, long_length, short_length)
    return jnp.where(jnp.arange(REQS) == full_request, CACHE, lengths).astype(jnp.int32)


def shard_levels(stream_key, extent, pieces, smallest, high):
    factor_of, own = 1.0, jax.random.fold_in(stream_key, 6)
    for axis_at, blocks in pieces:
        heights = jnp.exp(jax.random.uniform(jax.random.fold_in(own, axis_at), (blocks,), jnp.float32, smallest / len(pieces), high / len(pieces)))
        factor_of = factor_of * jnp.repeat(heights, extent[axis_at] // blocks).reshape([-1 if axis == axis_at else 1 for axis in range(len(extent))])
    return factor_of


def deal_out(own_key, own, number, rows, count, top, most, lean):
    order = jax.random.permutation(own_key, count)
    heavy_load, usual = load_shares(count, rows * top, most, lean, True), load_shares(count, rows * top, most, lean, False)
    places = jnp.arange(count)

    def named(sizes, rotation):
        used = int((sizes > 0).sum())
        fixed = max(1, used // 4)
        shifted = fixed + (places - fixed + rotation * (used - fixed)) % max(1, count - fixed)
        return jnp.zeros((count,), jnp.int32).at[order[jnp.where(places < fixed, places, shifted)]].set(jnp.asarray(sizes, jnp.int32))

    sizes = jnp.where(number % 4 == 0, named(heavy_load, number // 4), named(usual, number - number // 4 - 1))
    mixed = jax.random.permutation(jax.random.fold_in(own, 3), count)
    giver, taker = mixed[0:count // 2 * 2:2], mixed[1:count // 2 * 2:2]
    room = jnp.minimum(sizes[giver] - 1, most - sizes[taker]) // 2
    room = jnp.where((giver == order[0]) | (taker == order[0]) | (sizes[taker] == 0), 0, jnp.maximum(room, 0))
    shifted = jax.random.randint(jax.random.fold_in(own, 4), (count // 2,), 0, 1 << 20) % (room + 1)
    sizes = sizes.at[giver].add(-shifted).at[taker].add(shifted)
    items = jnp.searchsorted(jnp.cumsum(sizes), jnp.arange(rows * top), side="right").astype(jnp.int32)
    grid = items.reshape(top, rows).T
    grid = grid[jax.random.permutation(jax.random.fold_in(own, 1), rows)]
    rotation = jax.random.randint(jax.random.fold_in(own, 2), (rows, 1), 0, top)
    return jnp.take_along_axis(grid, (jnp.arange(top)[None, :] + rotation) % top, axis=1)


def load_shares(number_of, total, bound, skew, full):
    loads = [(1 << 20) // math.isqrt(rank ** skew) + 1 for rank in range(1, number_of + 1)]
    largest = bound if full else min(bound, max(-(-total // number_of), total * loads[0] // sum(loads)))
    least = 1 if total - largest >= number_of - 1 else 0
    counts, surplus = [largest] + [least] * (number_of - 1), total - largest - least * (number_of - 1)
    while surplus > 0:
        candidates = [i for i in range(1, number_of) if counts[i] < largest] or [i for i in range(1, number_of) if counts[i] < bound]
        mass, budget = sum([loads[i] for i in candidates]), surplus
        for i in candidates:
            addition = min(bound - counts[i], max(1, budget * loads[i] // mass), surplus)
            counts[i] = counts[i] + addition
            surplus = surplus - addition
    return np.array(counts)


def gaussian(key, dims, deviation, bound, split=(), kind=jnp.bfloat16):
    result = jax.random.normal(key, dims, jnp.float32) * deviation
    if len(split) > 0:
        result = shard_levels(key, dims, split, -0.22, 0.18) * result
    return jnp.clip(result, min=-bound, max=bound).astype(kind)


def setup_inputs(seed: int = 0) -> dict:
    key_of = jax.random.split(jax.random.key(seed), 16)
    queries = draw_queries(jax.random.fold_in(key_of[15], 71), 0)
    new_keys = gaussian(key_of[1], (REQS, STRETCH, D), 1.0, 6.0, ((0, 16), (1, 16)))
    new_values = gaussian(key_of[2], (REQS, STRETCH, D), 2.0, 12.0, ((0, 16), (1, 16)))
    cache_keys = draw_cache_keys(jax.random.fold_in(key_of[15], 71), 0)
    cache_values = gaussian(key_of[4], (REQS, CACHE, D), 2.0, 12.0, ((0, 16), (1, 16)))
    cache_lengths = draw_cache_lengths(jax.random.fold_in(key_of[15], 71), 0)
    relative_bias = gaussian(key_of[6], (H, BUCKETS), 1.0, 4.0, (), jnp.float32)
    residual = draw_residual(jax.random.fold_in(key_of[15], 71), 0)
    out_weight = gaussian(key_of[8], (D, D), D ** -0.5, 0.1875)
    norm_gain = jnp.clip(1.0 + 0.1 * jax.random.normal(key_of[9], (D,), jnp.float32), 0.5, 1.5).astype(jnp.bfloat16)
    router_weight = gaussian(key_of[10], (D, EXPERTS), D ** -0.5, 0.1875)
    routes_keys = jax.random.split(jax.random.fold_in(key_of[11], 1), REQS * STRETCH // Q_DEV)
    routes_turns = jax.random.permutation(jax.random.fold_in(key_of[11], 3), REQS * STRETCH // Q_DEV)
    routes = jax.vmap(lambda own, number: deal_out(jax.random.fold_in(key_of[11], 2), own, number, Q_DEV, EXPERTS, TOP, CAP, 2))(routes_keys, routes_turns).reshape((REQS, STRETCH, TOP))
    gate_weight = gaussian(key_of[12], (EXPERTS, D, FF), D ** -0.5, 0.1875, ((0, 16), (2, 16)))
    up_weight = gaussian(key_of[13], (EXPERTS, D, FF), D ** -0.5, 0.1875, ((0, 16), (2, 16)))
    down_weight = gaussian(key_of[14], (EXPERTS, D, FF), FF ** -0.5, 0.109375, ((0, 16), (2, 16)))
    return {"queries": queries, "new_keys": new_keys, "new_values": new_values, "cache_keys": cache_keys, "cache_values": cache_values, "cache_lengths": cache_lengths, "relative_bias": relative_bias, "residual": residual, "out_weight": out_weight, "norm_gain": norm_gain, "router_weight": router_weight, "routes": routes, "gate_weight": gate_weight, "up_weight": up_weight, "down_weight": down_weight}


def bucket_number(distance, bucket_count, reach_limit):
    exact_count = bucket_count // 2
    if distance < exact_count:
        return distance
    level_value = exact_count + int(np.floor(exact_count * np.log(distance / exact_count) / np.log(reach_limit / exact_count)))
    return min(bucket_count - 1, level_value)

def bucket_edges(bucket_count, reach_limit):
    edge_list = []
    for target in range(1, bucket_count):
        probe_value = 0
        while bucket_number(probe_value, bucket_count, reach_limit) < target:
            probe_value += 1
        edge_list.append(probe_value)
    return edge_list

def bucket_index(distance, edge_list):
    bucket_level = jnp.zeros(distance.shape, jnp.int32)
    for edge_value in edge_list:
        bucket_level = bucket_level + (distance >= edge_value).astype(jnp.int32)
    return bucket_level

def block_attention(query_rows, key_rows, value_rows, visible, bias_field):
    scores = jnp.einsum('qd,gkd->qgk', query_rows.astype(jnp.float32), key_rows.astype(jnp.float32)) / 8.0 + bias_field
    masked = jnp.where(visible, scores, -1e+30)
    block_peak = lax.optimization_barrier(jnp.max(masked, axis=2))
    weights = jnp.where(visible, jnp.exp(masked - block_peak[:, :, None]), 0.0)
    block_total = lax.optimization_barrier(jnp.sum(weights, axis=2))
    rounded_weights = weights.astype(jnp.bfloat16)
    numerator = jnp.einsum('qgk,gkd->qgd', rounded_weights.astype(jnp.float32), value_rows.astype(jnp.float32))
    block_out = (numerator / jnp.maximum(block_total, 1.0)[:, :, None]).astype(jnp.bfloat16)
    best_peak = lax.optimization_barrier(jnp.max(block_peak, axis=1))
    factor = jnp.exp(block_peak - best_peak[:, None]) * block_total
    weighted = jnp.einsum('qg,qgd->qd', factor, block_out.astype(jnp.float32))
    return (weighted / lax.optimization_barrier(jnp.sum(factor, axis=1))[:, None]).astype(jnp.bfloat16)

def reference(queries, new_keys, new_values, cache_keys, cache_values, cache_lengths, relative_bias, residual, out_weight, norm_gain, router_weight, routes, gate_weight, up_weight, down_weight):
    edge_list = bucket_edges(BUCKETS, MAXDIST)
    key_span = CACHE_DEV + Q_DEV

    def attend_request(operands):
        query_rows, new_key_rows, new_value_rows, key_rows, value_rows, length = operands
        key_blocks = jnp.concatenate([key_rows.reshape(N_CUTS, CACHE_DEV, D), new_key_rows.reshape(N_CUTS, Q_DEV, D)], axis=1)
        value_blocks = jnp.concatenate([value_rows.reshape(N_CUTS, CACHE_DEV, D), new_value_rows.reshape(N_CUTS, Q_DEV, D)], axis=1)
        block_ids = jnp.arange(N_CUTS, dtype=jnp.int32)[:, None]
        cache_slots = block_ids * CACHE_DEV + jnp.arange(CACHE_DEV, dtype=jnp.int32)[None, :]
        new_slots = block_ids * Q_DEV + jnp.arange(Q_DEV, dtype=jnp.int32)[None, :]
        key_pos = jnp.concatenate([cache_slots, length + new_slots], axis=1)
        key_live = jnp.concatenate([cache_slots < length, new_slots >= 0], axis=1)
        query_pos = length + jnp.arange(STRETCH, dtype=jnp.int32)
        visible = key_live[None, :, :] & (key_pos[None, :, :] <= query_pos[:, None, None])
        distance = jnp.maximum(query_pos[:, None, None] - key_pos[None, :, :], 0)
        bucket = bucket_index(distance, edge_list)
        head_queries = query_rows.reshape(STRETCH, H, HD).transpose(1, 0, 2)
        head_keys = key_blocks.reshape(N_CUTS, key_span, H, HD).transpose(2, 0, 1, 3)
        head_values = value_blocks.reshape(N_CUTS, key_span, H, HD).transpose(2, 0, 1, 3)

        def one_head(head_operands):
            head_query, head_key, head_value, bias_table = head_operands
            bias_field = jnp.take(bias_table, bucket)
            return block_attention(head_query, head_key, head_value, visible, bias_field)
        head_out = lax.map(one_head, (head_queries, head_keys, head_values, relative_bias))
        return head_out.transpose(1, 0, 2).reshape(STRETCH, D)
    attended = lax.map(attend_request, (queries, new_keys, new_values, cache_keys, cache_values, cache_lengths))
    hidden = residual.reshape(-1, D).astype(jnp.float32) + jnp.dot(attended.reshape(-1, D), out_weight, preferred_element_type=jnp.float32)
    inv_rms = lax.rsqrt(lax.optimization_barrier(jnp.mean(hidden * hidden, axis=1, keepdims=True)) + 1e-06)
    normed = (hidden * inv_rms * norm_gain.astype(jnp.float32)).astype(jnp.bfloat16)
    logits = jnp.dot(normed, router_weight, preferred_element_type=jnp.float32)
    flat_routes = routes.reshape(-1, TOP)
    gate_values = jax.nn.sigmoid(jnp.take_along_axis(logits, flat_routes, axis=1))
    block_count = flat_routes.shape[0] // Q_DEV
    block_routes = flat_routes.reshape(block_count, Q_DEV, TOP)
    onehot = (block_routes[:, :, :, None] == jnp.arange(EXPERTS, dtype=jnp.int32)[None, None, None, :]).astype(jnp.int32)
    named_count = lax.optimization_barrier(jnp.sum(onehot, axis=2, dtype=jnp.int32))
    earlier = jnp.cumsum(named_count, axis=1, dtype=jnp.int32) - named_count
    slot_number = lax.optimization_barrier(jnp.sum(onehot * earlier[:, :, None, :], axis=3, dtype=jnp.int32))
    block_ids = jnp.broadcast_to(jnp.arange(block_count, dtype=jnp.int32)[:, None, None], (block_count, Q_DEV, TOP))
    token_rows = jnp.broadcast_to(normed.reshape(block_count, Q_DEV, 1, D), (block_count, Q_DEV, TOP, D))
    expert_in = jnp.zeros((EXPERTS, block_count, CAP, D), jnp.bfloat16).at[block_routes, block_ids, slot_number].set(token_rows)
    slice_width = FF // N_CUTS

    def run_expert(operands):
        expert_rows, w_gate, w_up, w_down = operands
        flat_rows = expert_rows.reshape(-1, D)

        def add_slice(slice_index, running_sum):
            offset = (slice_index * slice_width).astype(jnp.int32)
            gate_piece = lax.dynamic_slice_in_dim(w_gate, offset, slice_width, 1)
            up_piece = lax.dynamic_slice_in_dim(w_up, offset, slice_width, 1)
            down_piece = lax.dynamic_slice_in_dim(w_down, offset, slice_width, 1)
            gate_act = jnp.dot(flat_rows, gate_piece, preferred_element_type=jnp.float32)
            up_act = jnp.dot(flat_rows, up_piece, preferred_element_type=jnp.float32)
            act_rows = (jax.nn.gelu(gate_act) * up_act).astype(jnp.bfloat16)
            slice_part = jnp.dot(act_rows, down_piece.T, preferred_element_type=jnp.float32).astype(jnp.bfloat16)
            return running_sum + lax.optimization_barrier(slice_part).astype(jnp.float32)
        summed = lax.fori_loop(0, N_CUTS, add_slice, jnp.zeros(flat_rows.shape, jnp.float32))
        return summed.astype(jnp.bfloat16).reshape(expert_rows.shape)
    expert_out = lax.map(run_expert, (expert_in, gate_weight, up_weight, down_weight))
    picked = expert_out[block_routes, block_ids, slot_number]
    combined = lax.optimization_barrier(jnp.sum(gate_values.reshape(block_count, Q_DEV, TOP, 1) * picked.astype(jnp.float32), axis=2))
    layer_out = hidden + combined.reshape(-1, D)
    return layer_out.astype(jnp.bfloat16).reshape(REQS, STRETCH, D)
```

```python
from functools import partial

import jax
import jax.numpy as jnp
import numpy as np
from jax import lax
from jax.sharding import PartitionSpec as P
from jax.experimental import pallas as pl
from jax.experimental.pallas import tpu as pltpu

MAXDIST = 128


def shortened(value):
    return jax.tree.map(lambda a: a.astype(jnp.bfloat16) if a.dtype == jnp.float32 else a, value)


def bucket_number(distance, bucket_count, reach_limit):
    exact_count = bucket_count // 2
    if distance < exact_count:
        return distance
    level_value = exact_count + int(
        np.floor(exact_count * np.log(distance / exact_count) / np.log(reach_limit / exact_count))
    )
    return min(bucket_count - 1, level_value)


def bucket_edges(bucket_count, reach_limit):
    edge_list = []
    for target in range(1, bucket_count):
        probe_value = 0
        while bucket_number(probe_value, bucket_count, reach_limit) < target:
            probe_value += 1
        edge_list.append(probe_value)
    return edge_list


def bucket_index(distance, edge_list):
    bucket_level = jnp.zeros(distance.shape, jnp.int32)
    for edge_value in edge_list:
        bucket_level = bucket_level + (distance >= edge_value).astype(jnp.int32)
    return bucket_level


def attention_kernel(scalars, q_ref, k_ref, v_ref, tc_ref, tn_ref, o_ref, peak_ref, total_ref):
    length = scalars[0]
    cut = scalars[1]
    block = pl.program_id(0)
    q_rows = q_ref.shape[0]
    head_count, key_span, head_dim = k_ref.shape
    cache_rows = tc_ref.shape[2] - q_rows
    new_rows = key_span - cache_rows
    row = lax.broadcasted_iota(jnp.int32, (q_rows, key_span), 0)
    col = lax.broadcasted_iota(jnp.int32, (q_rows, key_span), 1)
    cache_live = cut * cache_rows + col < length
    new_live = cut * new_rows + (col - cache_rows) <= block * q_rows + row
    is_cache = col < cache_rows
    visible = (is_cache & cache_live) | (jnp.logical_not(is_cache) & new_live)
    cache_width = tc_ref.shape[2]
    new_width = tn_ref.shape[2]
    for h in range(head_count):
        query = q_ref[:, h * head_dim:(h + 1) * head_dim]
        scores = lax.dot_general(
            query, k_ref[h], (((1,), (1,)), ((), ())), preferred_element_type=jnp.float32
        ) / 8.0
        cache_table = jnp.broadcast_to(tc_ref[0, h:h + 1, :], (q_rows, cache_width))
        cache_bias = pltpu.roll(cache_table, cache_width - q_rows, 1, stride=1, stride_axis=0)
        new_table = jnp.broadcast_to(tn_ref[0, h:h + 1, :], (q_rows, new_width))
        new_bias = pltpu.roll(new_table, new_width - q_rows, 1, stride=1, stride_axis=0)
        bias = jnp.concatenate([cache_bias[:, :cache_rows], new_bias[:, :new_rows]], axis=1)
        masked = jnp.where(visible, scores + bias, -1e30)
        peak = jnp.max(masked, axis=1, keepdims=True)
        weights = jnp.where(visible, jnp.exp(masked - peak), 0.0)
        total = jnp.sum(weights, axis=1, keepdims=True)
        numerator = jnp.dot(
            weights.astype(jnp.bfloat16), v_ref[h], preferred_element_type=jnp.float32
        )
        o_ref[:, h * head_dim:(h + 1) * head_dim] = (
            numerator / jnp.maximum(total, 1.0)
        ).astype(o_ref.dtype)
        peak_ref[:, h:h + 1] = peak
        total_ref[:, h:h + 1] = total


def bias_tables(tables, length, cut, q_rows, cache_rows, new_rows, query_blocks):
    edges = bucket_edges(tables.shape[1], MAXDIST)
    blocks = jnp.arange(query_blocks, dtype=jnp.int32)[:, None]
    cache_lanes = jnp.arange(cache_rows + q_rows, dtype=jnp.int32)[None, :]
    new_lanes = jnp.arange(new_rows + q_rows, dtype=jnp.int32)[None, :]
    cache_distance = length + blocks * q_rows - cut * cache_rows + q_rows - cache_lanes
    new_distance = (blocks * q_rows - cut * new_rows) + q_rows - new_lanes
    cache_bucket = bucket_index(jnp.maximum(cache_distance, 0), edges)
    new_bucket = bucket_index(jnp.maximum(new_distance, 0), edges)
    cache_table = jnp.take(tables, cache_bucket, axis=1).transpose(1, 0, 2)
    new_table = jnp.take(tables, new_bucket, axis=1).transpose(1, 0, 2)
    return cache_table, new_table


def block_partials(query_rows, key_rows, value_rows, tables, length, cut, cache_rows, q_rows):
    head_count = tables.shape[0]
    model_width = query_rows.shape[1]
    head_dim = model_width // head_count
    key_span = key_rows.shape[0]
    new_rows = key_span - cache_rows
    query_total = query_rows.shape[0]
    query_blocks = query_total // q_rows
    head_keys = key_rows.reshape(key_span, head_count, head_dim).transpose(1, 0, 2)
    head_values = value_rows.reshape(key_span, head_count, head_dim).transpose(1, 0, 2)
    cache_table, new_table = bias_tables(
        tables, length, cut, q_rows, cache_rows, new_rows, query_blocks
    )
    scalars = jnp.stack([length, cut]).astype(jnp.int32)
    grid_spec = pltpu.PrefetchScalarGridSpec(
        num_scalar_prefetch=1,
        grid=(query_blocks,),
        in_specs=[
            pl.BlockSpec((q_rows, model_width), lambda b, s: (b, 0)),
            pl.BlockSpec((head_count, key_span, head_dim), lambda b, s: (0, 0, 0)),
            pl.BlockSpec((head_count, key_span, head_dim), lambda b, s: (0, 0, 0)),
            pl.BlockSpec((1, head_count, cache_table.shape[2]), lambda b, s: (b, 0, 0)),
            pl.BlockSpec((1, head_count, new_table.shape[2]), lambda b, s: (b, 0, 0)),
        ],
        out_specs=[
            pl.BlockSpec((q_rows, model_width), lambda b, s: (b, 0)),
            pl.BlockSpec((q_rows, head_count), lambda b, s: (b, 0)),
            pl.BlockSpec((q_rows, head_count), lambda b, s: (b, 0)),
        ],
    )
    pairs = query_total * key_span * head_count
    return pl.pallas_call(
        attention_kernel,
        grid_spec=grid_spec,
        out_shape=[
            jax.ShapeDtypeStruct((query_total, model_width), jnp.bfloat16),
            jax.ShapeDtypeStruct((query_total, head_count), jnp.float32),
            jax.ShapeDtypeStruct((query_total, head_count), jnp.float32),
        ],
        cost_estimate=pl.CostEstimate(
            flops=4 * pairs * head_dim,
            transcendentals=pairs,
            bytes_accessed=4 * query_total * model_width + 4 * key_span * model_width,
        ),
    )(scalars, query_rows, head_keys, head_values, cache_table, new_table)


def merge_blocks(block_out, block_peak, block_total):
    best_peak = jnp.max(block_peak, axis=0)
    factor = jnp.exp(block_peak - best_peak[None]) * block_total
    weighted = jnp.sum(factor[..., None] * block_out.astype(jnp.float32), axis=0)
    return (weighted / jnp.sum(factor, axis=0)[..., None]).astype(jnp.bfloat16)


def expert_part(row_block, gate_piece, up_piece, down_piece):
    gate_act = jnp.einsum(
        "necd,edf->necf", row_block, gate_piece, preferred_element_type=jnp.float32
    )
    up_act = jnp.einsum("necd,edf->necf", row_block, up_piece, preferred_element_type=jnp.float32)
    act_rows = (jax.nn.gelu(gate_act) * up_act).astype(jnp.bfloat16)
    return jnp.einsum("necf,edf->necd", act_rows, down_piece, preferred_element_type=jnp.float32)


def per_device(
    queries,
    new_keys,
    new_values,
    cache_keys,
    cache_values,
    cache_lengths,
    relative_bias,
    residual,
    out_weight,
    norm_gain,
    router_weight,
    routes,
    gate_weight,
    up_weight,
    down_weight,
):
    cut_count = lax.axis_size("cuts")
    cut_index = lax.axis_index("cuts")
    q_rows = queries.shape[1]
    cache_rows = cache_keys.shape[1]
    model_width = queries.shape[2]
    head_count = relative_bias.shape[0]
    head_dim = model_width // head_count
    bucket_count = relative_bias.shape[1]
    length = cache_lengths[0]
    query_total = q_rows * cut_count
    local_keys = jnp.concatenate([cache_keys[0], new_keys[0]], axis=0)
    local_values = jnp.concatenate([cache_values[0], new_values[0]], axis=0)
    every_query = lax.all_gather(queries[0], "cuts", axis=0, tiled=True)
    block_out, block_peak, block_total = block_partials(
        every_query, local_keys, local_values, relative_bias, length, cut_index, cache_rows, q_rows
    )
    block_out = block_out.reshape(cut_count, q_rows, model_width)
    block_peak = block_peak.reshape(cut_count, q_rows, head_count)
    block_total = block_total.reshape(cut_count, q_rows, head_count)
    block_out = lax.all_to_all(
        shortened(block_out), "cuts", split_axis=0, concat_axis=0, tiled=True
    ).astype(block_out.dtype)
    block_peak, block_total = (
        lax.all_to_all(
            shortened(block_peak), "cuts", split_axis=0, concat_axis=0, tiled=True
        ).astype(block_peak.dtype),
        lax.all_to_all(
            shortened(block_total), "cuts", split_axis=0, concat_axis=0, tiled=True
        ).astype(block_total.dtype),
    )
    block_out = block_out.reshape(cut_count, q_rows, head_count, head_dim)
    attended = merge_blocks(block_out, block_peak, block_total).reshape(q_rows, model_width)
    hidden = residual[0].astype(jnp.float32) + jnp.dot(
        attended, out_weight, preferred_element_type=jnp.float32
    )
    inv_rms = lax.rsqrt(jnp.mean(hidden * hidden, axis=1, keepdims=True) + 1e-06)
    normed = (hidden * inv_rms * norm_gain.astype(jnp.float32)).astype(jnp.bfloat16)
    experts = router_weight.shape[1]
    capacity = (10 * q_rows + 4 * experts - 1) // (4 * experts)
    logits = jnp.dot(normed, router_weight, preferred_element_type=jnp.float32)
    chosen = routes[0]
    onehot = (chosen[:, :, None] == jnp.arange(experts, dtype=jnp.int32)[None, None, :]).astype(
        jnp.float32
    )
    gate_values = jax.nn.sigmoid(jnp.sum(onehot * logits[:, None, :], axis=2))
    named_count = jnp.sum(onehot, axis=1)
    earlier_mask = (jnp.arange(q_rows)[:, None] > jnp.arange(q_rows)[None, :]).astype(jnp.bfloat16)
    earlier = jnp.dot(
        earlier_mask, named_count.astype(jnp.bfloat16), preferred_element_type=jnp.float32
    )
    slot_number = jnp.sum(onehot * earlier[:, None, :], axis=2)
    slot_hot = (
        slot_number[:, :, None] == jnp.arange(capacity, dtype=jnp.float32)[None, None, :]
    ).astype(jnp.float32)
    dispatch = jnp.einsum("tke,tkc->ect", onehot, slot_hot)
    buffers = jnp.einsum(
        "ect,td->ecd", dispatch.astype(jnp.bfloat16), normed, preferred_element_type=jnp.float32
    ).astype(jnp.bfloat16)
    arrived = lax.all_to_all(buffers, "req", split_axis=0, concat_axis=0, tiled=True)
    local_experts = gate_weight.shape[0]
    gathered = lax.all_gather(arrived, "cuts", axis=0, tiled=True)
    row_count = lax.axis_size("cuts") * arrived.shape[0]
    row_block = gathered.reshape(row_count, local_experts, capacity, model_width)
    expert_out = lax.psum_scatter(
        expert_part(row_block, gate_weight, up_weight, down_weight)
        .reshape(row_count, local_experts * capacity, model_width)
        .astype(jnp.bfloat16),
        "cuts",
        scatter_dimension=0,
        tiled=True,
    )
    returned = lax.all_to_all(expert_out, "req", split_axis=0, concat_axis=0, tiled=True)
    combine = jnp.einsum(
        "tke,tkc,tk->ect", onehot, slot_hot, gate_values, precision=lax.Precision.HIGHEST
    )
    gathered_back = jnp.einsum(
        "ect,ecd->td", combine, returned.astype(jnp.float32), precision=lax.Precision.HIGHEST
    )
    layer_out = hidden + gathered_back
    return layer_out.astype(jnp.bfloat16)[None]


def solution(mesh):
    return jax.shard_map(
        per_device,
        mesh=mesh,
        in_specs=(
            P("req", "cuts", None),
            P("req", "cuts", None),
            P("req", "cuts", None),
            P("req", "cuts", None),
            P("req", "cuts", None),
            P("req"),
            P(),
            P("req", "cuts", None),
            P(),
            P(),
            P(),
            P("req", "cuts", None),
            P("req", None, "cuts"),
            P("req", None, "cuts"),
            P("req", None, "cuts"),
        ),
        out_specs=P("req", "cuts", None),
        check_vma=False,
    )
```

```python
from functools import partial

import jax
import jax.numpy as jnp
import numpy as np
from jax import lax
from jax.sharding import PartitionSpec as P
from jax.experimental import pallas as pl
from jax.experimental.pallas import tpu as pltpu

MAXDIST = 128


def shortened(value):
    return jax.tree.map(lambda a: a.astype(jnp.bfloat16) if a.dtype == jnp.float32 else a, value)


def bucket_number(distance, bucket_count, reach_limit):
    exact_count = bucket_count // 2
    if distance < exact_count:
        return distance
    level_value = exact_count + int(
        np.floor(exact_count * np.log(distance / exact_count) / np.log(reach_limit / exact_count))
    )
    return min(bucket_count - 1, level_value)


def bucket_edges(bucket_count, reach_limit):
    edge_list = []
    for target in range(1, bucket_count):
        probe_value = 0
        while bucket_number(probe_value, bucket_count, reach_limit) < target:
            probe_value += 1
        edge_list.append(probe_value)
    return edge_list


def bucket_index(distance, edge_list):
    bucket_level = jnp.zeros(distance.shape, jnp.int32)
    for edge_value in edge_list:
        bucket_level = bucket_level + (distance >= edge_value).astype(jnp.int32)
    return bucket_level


def attention_kernel(scalars, q_ref, k_ref, v_ref, tc_ref, tn_ref, o_ref, peak_ref, total_ref):
    length = scalars[0]
    cut = scalars[1]
    block = pl.program_id(0)
    q_rows = q_ref.shape[0]
    head_count, key_span, head_dim = k_ref.shape
    cache_rows = tc_ref.shape[2] - q_rows
    new_rows = key_span - cache_rows
    row = lax.broadcasted_iota(jnp.int32, (q_rows, key_span), 0)
    col = lax.broadcasted_iota(jnp.int32, (q_rows, key_span), 1)
    cache_live = cut * cache_rows + col < length
    new_live = cut * new_rows + (col - cache_rows) <= block * q_rows + row
    is_cache = col < cache_rows
    visible = (is_cache & cache_live) | (jnp.logical_not(is_cache) & new_live)
    cache_width = tc_ref.shape[2]
    new_width = tn_ref.shape[2]
    for h in range(head_count):
        query = q_ref[:, h * head_dim:(h + 1) * head_dim]
        scores = lax.dot_general(
            query, k_ref[h], (((1,), (1,)), ((), ())), preferred_element_type=jnp.float32
        ) / 8.0
        cache_table = jnp.broadcast_to(tc_ref[0, h:h + 1, :], (q_rows, cache_width))
        cache_bias = pltpu.roll(cache_table, cache_width - q_rows, 1, stride=1, stride_axis=0)
        new_table = jnp.broadcast_to(tn_ref[0, h:h + 1, :], (q_rows, new_width))
        new_bias = pltpu.roll(new_table, new_width - q_rows, 1, stride=1, stride_axis=0)
        bias = jnp.concatenate([cache_bias[:, :cache_rows], new_bias[:, :new_rows]], axis=1)
        masked = jnp.where(visible, scores + bias, -1e30)
        peak = jnp.max(masked, axis=1, keepdims=True)
        weights = jnp.where(visible, jnp.exp(masked - peak), 0.0)
        total = jnp.sum(weights, axis=1, keepdims=True)
        numerator = jnp.dot(
            weights.astype(jnp.bfloat16), v_ref[h], preferred_element_type=jnp.float32
        )
        o_ref[:, h * head_dim:(h + 1) * head_dim] = (
            numerator / jnp.maximum(total, 1.0)
        ).astype(o_ref.dtype)
        peak_ref[:, h:h + 1] = peak
        total_ref[:, h:h + 1] = total


def bias_tables(tables, length, cut, q_rows, cache_rows, new_rows, query_blocks):
    edges = bucket_edges(tables.shape[1], MAXDIST)
    blocks = jnp.arange(query_blocks, dtype=jnp.int32)[:, None]
    cache_lanes = jnp.arange(cache_rows + q_rows, dtype=jnp.int32)[None, :]
    new_lanes = jnp.arange(new_rows + q_rows, dtype=jnp.int32)[None, :]
    cache_distance = length + blocks * q_rows - cut * cache_rows + q_rows - cache_lanes
    new_distance = (blocks * q_rows - cut * new_rows) + q_rows - new_lanes
    cache_bucket = bucket_index(jnp.maximum(cache_distance, 0), edges)
    new_bucket = bucket_index(jnp.maximum(new_distance, 0), edges)
    choices = jnp.arange(tables.shape[1], dtype=jnp.int32)
    cache_hot = (cache_bucket[..., None] == choices).astype(jnp.float32)
    new_hot = (new_bucket[..., None] == choices).astype(jnp.float32)
    cache_table = jnp.einsum("bmk,hk->bhm", cache_hot, tables, precision=lax.Precision.HIGHEST)
    new_table = jnp.einsum("bmk,hk->bhm", new_hot, tables, precision=lax.Precision.HIGHEST)
    return cache_table, new_table


def block_partials(query_rows, key_rows, value_rows, tables, length, cut, cache_rows, q_rows):
    head_count = tables.shape[0]
    model_width = query_rows.shape[1]
    head_dim = model_width // head_count
    key_span = key_rows.shape[0]
    new_rows = key_span - cache_rows
    query_total = query_rows.shape[0]
    query_blocks = query_total // q_rows
    head_keys = key_rows.reshape(key_span, head_count, head_dim).transpose(1, 0, 2)
    head_values = value_rows.reshape(key_span, head_count, head_dim).transpose(1, 0, 2)
    cache_table, new_table = bias_tables(
        tables, length, cut, q_rows, cache_rows, new_rows, query_blocks
    )
    scalars = jnp.stack([length, cut]).astype(jnp.int32)
    grid_spec = pltpu.PrefetchScalarGridSpec(
        num_scalar_prefetch=1,
        grid=(query_blocks,),
        in_specs=[
            pl.BlockSpec((q_rows, model_width), lambda b, s: (b, 0)),
            pl.BlockSpec((head_count, key_span, head_dim), lambda b, s: (0, 0, 0)),
            pl.BlockSpec((head_count, key_span, head_dim), lambda b, s: (0, 0, 0)),
            pl.BlockSpec((1, head_count, cache_table.shape[2]), lambda b, s: (b, 0, 0)),
            pl.BlockSpec((1, head_count, new_table.shape[2]), lambda b, s: (b, 0, 0)),
        ],
        out_specs=[
            pl.BlockSpec((q_rows, model_width), lambda b, s: (b, 0)),
            pl.BlockSpec((q_rows, head_count), lambda b, s: (b, 0)),
            pl.BlockSpec((q_rows, head_count), lambda b, s: (b, 0)),
        ],
    )
    pairs = query_total * key_span * head_count
    return pl.pallas_call(
        attention_kernel,
        grid_spec=grid_spec,
        out_shape=[
            jax.ShapeDtypeStruct((query_total, model_width), jnp.bfloat16),
            jax.ShapeDtypeStruct((query_total, head_count), jnp.float32),
            jax.ShapeDtypeStruct((query_total, head_count), jnp.float32),
        ],
        cost_estimate=pl.CostEstimate(
            flops=4 * pairs * head_dim,
            transcendentals=pairs,
            bytes_accessed=4 * query_total * model_width + 4 * key_span * model_width,
        ),
    )(scalars, query_rows, head_keys, head_values, cache_table, new_table)


def merge_blocks(block_out, block_peak, block_total):
    best_peak = jnp.max(block_peak, axis=0)
    factor = jnp.exp(block_peak - best_peak[None]) * block_total
    weighted = jnp.sum(factor[..., None] * block_out.astype(jnp.float32), axis=0)
    return (weighted / jnp.sum(factor, axis=0)[..., None]).astype(jnp.bfloat16)


def per_device(
    queries,
    new_keys,
    new_values,
    cache_keys,
    cache_values,
    cache_lengths,
    relative_bias,
    residual,
    out_weight,
    norm_gain,
    router_weight,
    routes,
    gate_weight,
    up_weight,
    down_weight,
):
    cut_count = lax.axis_size("cuts")
    cut_index = lax.axis_index("cuts")
    q_rows = queries.shape[1]
    cache_rows = cache_keys.shape[1]
    model_width = queries.shape[2]
    head_count = relative_bias.shape[0]
    head_dim = model_width // head_count
    bucket_count = relative_bias.shape[1]
    length = cache_lengths[0]
    query_total = q_rows * cut_count
    local_keys = jnp.concatenate([cache_keys[0], new_keys[0]], axis=0)
    local_values = jnp.concatenate([cache_values[0], new_values[0]], axis=0)
    every_query = lax.all_gather(queries[0], "cuts", axis=0, tiled=True)
    block_out, block_peak, block_total = block_partials(
        every_query, local_keys, local_values, relative_bias, length, cut_index, cache_rows, q_rows
    )
    block_out = block_out.reshape(cut_count, q_rows, model_width)
    block_peak = block_peak.reshape(cut_count, q_rows, head_count)
    block_total = block_total.reshape(cut_count, q_rows, head_count)
    block_out = lax.all_to_all(
        shortened(block_out), "cuts", split_axis=0, concat_axis=0, tiled=True
    ).astype(block_out.dtype)
    block_peak, block_total = (
        lax.all_to_all(
            shortened(block_peak), "cuts", split_axis=0, concat_axis=0, tiled=True
        ).astype(block_peak.dtype),
        lax.all_to_all(
            shortened(block_total), "cuts", split_axis=0, concat_axis=0, tiled=True
        ).astype(block_total.dtype),
    )
    block_out = block_out.reshape(cut_count, q_rows, head_count, head_dim)
    attended = merge_blocks(block_out, block_peak, block_total).reshape(q_rows, model_width)
    hidden = residual[0].astype(jnp.float32) + jnp.dot(
        attended, out_weight, preferred_element_type=jnp.float32
    )
    inv_rms = lax.rsqrt(jnp.mean(hidden * hidden, axis=1, keepdims=True) + 1e-06)
    normed = (hidden * inv_rms * norm_gain.astype(jnp.float32)).astype(jnp.bfloat16)
    experts = router_weight.shape[1]
    capacity = (10 * q_rows + 4 * experts - 1) // (4 * experts)
    logits = jnp.dot(normed, router_weight, preferred_element_type=jnp.float32)
    chosen = routes[0]
    onehot = (chosen[:, :, None] == jnp.arange(experts, dtype=jnp.int32)[None, None, :]).astype(
        jnp.float32
    )
    gate_values = jax.nn.sigmoid(jnp.sum(onehot * logits[:, None, :], axis=2))
    named_count = jnp.sum(onehot, axis=1)
    earlier_mask = (jnp.arange(q_rows)[:, None] > jnp.arange(q_rows)[None, :]).astype(jnp.bfloat16)
    earlier = jnp.dot(
        earlier_mask, named_count.astype(jnp.bfloat16), preferred_element_type=jnp.float32
    )
    slot_number = jnp.sum(onehot * earlier[:, None, :], axis=2)
    slot_hot = (
        slot_number[:, :, None] == jnp.arange(capacity, dtype=jnp.float32)[None, None, :]
    ).astype(jnp.float32)
    dispatch = jnp.einsum("tke,tkc->ect", onehot, slot_hot)
    buffers = jnp.einsum(
        "ect,td->ecd", dispatch.astype(jnp.bfloat16), normed, preferred_element_type=jnp.float32
    ).astype(jnp.bfloat16)
    arrived = lax.all_to_all(buffers, "req", split_axis=0, concat_axis=0, tiled=True)
    full_gate = lax.all_gather(gate_weight[0], "cuts", axis=1, tiled=True)
    full_up = lax.all_gather(up_weight[0], "cuts", axis=1, tiled=True)
    full_down = lax.all_gather(down_weight[0], "cuts", axis=1, tiled=True)
    flat_rows = arrived.reshape(-1, model_width)
    gate_act = jnp.dot(flat_rows, full_gate, preferred_element_type=jnp.float32)
    up_act = jnp.dot(flat_rows, full_up, preferred_element_type=jnp.float32)
    act_rows = (jax.nn.gelu(gate_act) * up_act).astype(jnp.bfloat16)
    expert_out = lax.dot_general(
        act_rows, full_down, (((1,), (1,)), ((), ())), preferred_element_type=jnp.float32
    ).astype(jnp.bfloat16).reshape(arrived.shape)
    returned = lax.all_to_all(expert_out, "req", split_axis=0, concat_axis=0, tiled=True)
    combine = jnp.einsum(
        "tke,tkc,tk->ect", onehot, slot_hot, gate_values, precision=lax.Precision.HIGHEST
    )
    gathered_back = jnp.einsum(
        "ect,ecd->td", combine, returned.astype(jnp.float32), precision=lax.Precision.HIGHEST
    )
    layer_out = hidden + gathered_back
    return layer_out.astype(jnp.bfloat16)[None]


def solution(mesh):
    return jax.shard_map(
        per_device,
        mesh=mesh,
        in_specs=(
            P("req", "cuts", None),
            P("req", "cuts", None),
            P("req", "cuts", None),
            P("req", "cuts", None),
            P("req", "cuts", None),
            P("req"),
            P(),
            P("req", "cuts", None),
            P(),
            P(),
            P(),
            P("req", "cuts", None),
            P("req", None, "cuts"),
            P("req", None, "cuts"),
            P("req", None, "cuts"),
        ),
        out_specs=P("req", "cuts", None),
        check_vma=False,
    )
```

```python
from functools import partial

import jax
import jax.numpy as jnp
import numpy as np
from jax import lax
from jax.sharding import PartitionSpec as P
from jax.experimental import pallas as pl
from jax.experimental.pallas import tpu as pltpu

MAXDIST = 128


def shortened(value):
    return jax.tree.map(lambda a: a.astype(jnp.bfloat16) if a.dtype == jnp.float32 else a, value)


def bucket_number(distance, bucket_count, reach_limit):
    exact_count = bucket_count // 2
    if distance < exact_count:
        return distance
    level_value = exact_count + int(
        np.floor(exact_count * np.log(distance / exact_count) / np.log(reach_limit / exact_count))
    )
    return min(bucket_count - 1, level_value)


def bucket_edges(bucket_count, reach_limit):
    edge_list = []
    for target in range(1, bucket_count):
        probe_value = 0
        while bucket_number(probe_value, bucket_count, reach_limit) < target:
            probe_value += 1
        edge_list.append(probe_value)
    return edge_list


def bucket_index(distance, edge_list):
    bucket_level = jnp.zeros(distance.shape, jnp.int32)
    for edge_value in edge_list:
        bucket_level = bucket_level + (distance >= edge_value).astype(jnp.int32)
    return bucket_level


def attention_kernel(scalars, q_ref, k_ref, v_ref, tc_ref, tn_ref, o_ref):
    length = scalars[0]
    block = pl.program_id(0)
    q_rows = q_ref.shape[0]
    key_blocks, key_span, head_dim = k_ref.shape
    cache_rows = tc_ref.shape[2] - q_rows
    new_rows = key_span - cache_rows
    row = lax.broadcasted_iota(jnp.int32, (q_rows, key_span), 0)
    col = lax.broadcasted_iota(jnp.int32, (q_rows, key_span), 1)
    is_cache = col < cache_rows
    cache_width = tc_ref.shape[2]
    new_width = tn_ref.shape[2]
    query = q_ref[...]

    def one_block(g, carry):
        best, weighted, factor_sum = carry
        cache_live = g * cache_rows + col < length
        new_live = g * new_rows + (col - cache_rows) <= block * q_rows + row
        visible = (is_cache & cache_live) | (jnp.logical_not(is_cache) & new_live)
        scores = lax.dot_general(
            query, k_ref[g], (((1,), (1,)), ((), ())), preferred_element_type=jnp.float32
        ) / 8.0
        cache_table = jnp.broadcast_to(tc_ref[0, pl.ds(g, 1), :], (q_rows, cache_width))
        cache_bias = pltpu.roll(cache_table, cache_width - q_rows, 1, stride=1, stride_axis=0)
        new_table = jnp.broadcast_to(tn_ref[0, pl.ds(g, 1), :], (q_rows, new_width))
        new_bias = pltpu.roll(new_table, new_width - q_rows, 1, stride=1, stride_axis=0)
        bias = jnp.concatenate([cache_bias[:, :cache_rows], new_bias[:, :new_rows]], axis=1)
        masked = jnp.where(visible, scores + bias, -1e30)
        peak = jnp.max(masked, axis=1, keepdims=True)
        weights = jnp.where(visible, jnp.exp(masked - peak), 0.0)
        total = jnp.sum(weights, axis=1, keepdims=True)
        numerator = jnp.dot(
            weights.astype(jnp.bfloat16), v_ref[g], preferred_element_type=jnp.float32
        )
        block_out = (numerator / jnp.maximum(total, 1.0)).astype(jnp.bfloat16).astype(jnp.float32)
        new_best = jnp.maximum(best, peak)
        rescale = jnp.exp(best - new_best)
        factor = jnp.exp(peak - new_best) * total
        return (new_best, weighted * rescale + factor * block_out, factor_sum * rescale + factor)

    start = (
        jnp.full((q_rows, 1), -1e30, jnp.float32),
        jnp.zeros((q_rows, head_dim), jnp.float32),
        jnp.zeros((q_rows, 1), jnp.float32),
    )
    best, weighted, factor_sum = lax.fori_loop(0, key_blocks, one_block, start)
    o_ref[...] = (weighted / factor_sum).astype(o_ref.dtype)


def bias_tables(head_table, length, q_rows, cache_rows, new_rows, query_blocks, key_blocks):
    edges = bucket_edges(head_table.shape[1], MAXDIST)
    blocks = jnp.arange(query_blocks, dtype=jnp.int32)[:, None, None]
    key_ids = jnp.arange(key_blocks, dtype=jnp.int32)[None, :, None]
    cache_lanes = jnp.arange(cache_rows + q_rows, dtype=jnp.int32)[None, None, :]
    new_lanes = jnp.arange(new_rows + q_rows, dtype=jnp.int32)[None, None, :]
    cache_distance = length + blocks * q_rows - key_ids * cache_rows + q_rows - cache_lanes
    new_distance = (blocks * q_rows - key_ids * new_rows) + q_rows - new_lanes
    cache_bucket = bucket_index(jnp.maximum(cache_distance, 0), edges)
    new_bucket = bucket_index(jnp.maximum(new_distance, 0), edges)
    choices = jnp.arange(head_table.shape[1], dtype=jnp.int32)
    cache_hot = (cache_bucket[..., None] == choices).astype(jnp.float32)
    new_hot = (new_bucket[..., None] == choices).astype(jnp.float32)
    cache_table = jnp.einsum("agmk,hk->agm", cache_hot, head_table, precision=lax.Precision.HIGHEST)
    new_table = jnp.einsum("agmk,hk->agm", new_hot, head_table, precision=lax.Precision.HIGHEST)
    return cache_table, new_table


def block_partials(query_rows, key_rows, value_rows, head_table, length, cache_rows, q_rows):
    key_blocks, key_span, head_dim = key_rows.shape
    new_rows = key_span - cache_rows
    query_total = query_rows.shape[0]
    query_blocks = query_total // q_rows
    cache_table, new_table = bias_tables(
        head_table, length, q_rows, cache_rows, new_rows, query_blocks, key_blocks
    )
    scalars = jnp.stack([length]).astype(jnp.int32)
    grid_spec = pltpu.PrefetchScalarGridSpec(
        num_scalar_prefetch=1,
        grid=(query_blocks,),
        in_specs=[
            pl.BlockSpec((q_rows, head_dim), lambda b, s: (b, 0)),
            pl.BlockSpec((key_blocks, key_span, head_dim), lambda b, s: (0, 0, 0)),
            pl.BlockSpec((key_blocks, key_span, head_dim), lambda b, s: (0, 0, 0)),
            pl.BlockSpec((1, key_blocks, cache_table.shape[2]), lambda b, s: (b, 0, 0)),
            pl.BlockSpec((1, key_blocks, new_table.shape[2]), lambda b, s: (b, 0, 0)),
        ],
        out_specs=pl.BlockSpec((q_rows, head_dim), lambda b, s: (b, 0)),
    )
    pairs = query_total * key_span * key_blocks
    return pl.pallas_call(
        attention_kernel,
        grid_spec=grid_spec,
        out_shape=jax.ShapeDtypeStruct((query_total, head_dim), jnp.bfloat16),
        cost_estimate=pl.CostEstimate(
            flops=4 * pairs * head_dim,
            transcendentals=pairs,
            bytes_accessed=4 * query_total * head_dim * key_blocks + 4 * key_span * key_blocks * head_dim,
        ),
    )(scalars, query_rows, key_rows, value_rows, cache_table, new_table)


def per_device(
    queries,
    new_keys,
    new_values,
    cache_keys,
    cache_values,
    cache_lengths,
    relative_bias,
    residual,
    out_weight,
    norm_gain,
    router_weight,
    routes,
    gate_weight,
    up_weight,
    down_weight,
):
    cut_count = lax.axis_size("cuts")
    cut_index = lax.axis_index("cuts")
    q_rows = queries.shape[1]
    cache_rows = cache_keys.shape[1]
    model_width = queries.shape[2]
    head_count = relative_bias.shape[0]
    head_dim = model_width // head_count
    bucket_count = relative_bias.shape[1]
    length = cache_lengths[0]
    query_total = q_rows * cut_count
    local_keys = jnp.concatenate([cache_keys[0], new_keys[0]], axis=0)
    local_values = jnp.concatenate([cache_values[0], new_values[0]], axis=0)
    head_queries = lax.all_to_all(
        queries[0].reshape(q_rows, head_count, head_dim), "cuts", split_axis=1, concat_axis=0, tiled=True
    ).reshape(query_total, head_dim)
    key_span = local_keys.shape[0]
    head_keys = lax.all_to_all(
        local_keys.reshape(key_span, head_count, head_dim), "cuts", split_axis=1, concat_axis=0, tiled=True
    ).reshape(cut_count, key_span, head_dim)
    head_values = lax.all_to_all(
        local_values.reshape(key_span, head_count, head_dim), "cuts", split_axis=1, concat_axis=0, tiled=True
    ).reshape(cut_count, key_span, head_dim)
    head_table = lax.dynamic_slice_in_dim(relative_bias, cut_index, 1, 0)
    head_out = block_partials(
        head_queries, head_keys, head_values, head_table, length, cache_rows, q_rows
    )
    attended = lax.all_to_all(
        head_out.reshape(cut_count, q_rows, head_dim), "cuts", split_axis=0, concat_axis=0, tiled=True
    ).transpose(1, 0, 2).reshape(q_rows, model_width)
    hidden = residual[0].astype(jnp.float32) + jnp.dot(
        attended, out_weight, preferred_element_type=jnp.float32
    )
    inv_rms = lax.rsqrt(jnp.mean(hidden * hidden, axis=1, keepdims=True) + 1e-06)
    normed = (hidden * inv_rms * norm_gain.astype(jnp.float32)).astype(jnp.bfloat16)
    experts = router_weight.shape[1]
    capacity = (10 * q_rows + 4 * experts - 1) // (4 * experts)
    logits = jnp.dot(normed, router_weight, preferred_element_type=jnp.float32)
    chosen = routes[0]
    onehot = (chosen[:, :, None] == jnp.arange(experts, dtype=jnp.int32)[None, None, :]).astype(
        jnp.float32
    )
    gate_values = jax.nn.sigmoid(jnp.sum(onehot * logits[:, None, :], axis=2))
    named_count = jnp.sum(onehot, axis=1)
    earlier_mask = (jnp.arange(q_rows)[:, None] > jnp.arange(q_rows)[None, :]).astype(jnp.bfloat16)
    earlier = jnp.dot(
        earlier_mask, named_count.astype(jnp.bfloat16), preferred_element_type=jnp.float32
    )
    slot_number = jnp.sum(onehot * earlier[:, None, :], axis=2)
    slot_hot = (
        slot_number[:, :, None] == jnp.arange(capacity, dtype=jnp.float32)[None, None, :]
    ).astype(jnp.float32)
    dispatch = jnp.einsum("tke,tkc->ect", onehot, slot_hot)
    buffers = jnp.einsum(
        "ect,td->ecd", dispatch.astype(jnp.bfloat16), normed, preferred_element_type=jnp.float32
    ).astype(jnp.bfloat16)
    arrived = lax.all_to_all(buffers, "req", split_axis=0, concat_axis=0, tiled=True)
    full_gate = lax.all_gather(gate_weight[0], "cuts", axis=1, tiled=True)
    full_up = lax.all_gather(up_weight[0], "cuts", axis=1, tiled=True)
    full_down = lax.all_gather(down_weight[0], "cuts", axis=1, tiled=True)
    flat_rows = arrived.reshape(-1, model_width)
    gate_act = jnp.dot(flat_rows, full_gate, preferred_element_type=jnp.float32)
    up_act = jnp.dot(flat_rows, full_up, preferred_element_type=jnp.float32)
    act_rows = (jax.nn.gelu(gate_act) * up_act).astype(jnp.bfloat16)
    expert_out = lax.dot_general(
        act_rows, full_down, (((1,), (1,)), ((), ())), preferred_element_type=jnp.float32
    ).astype(jnp.bfloat16).reshape(arrived.shape)
    returned = lax.all_to_all(expert_out, "req", split_axis=0, concat_axis=0, tiled=True)
    combine = jnp.einsum(
        "tke,tkc,tk->ect", onehot, slot_hot, gate_values, precision=lax.Precision.HIGHEST
    )
    gathered_back = jnp.einsum(
        "ect,ecd->td", combine, returned.astype(jnp.float32), precision=lax.Precision.HIGHEST
    )
    layer_out = hidden + gathered_back
    return layer_out.astype(jnp.bfloat16)[None]


def solution(mesh):
    return jax.shard_map(
        per_device,
        mesh=mesh,
        in_specs=(
            P("req", "cuts", None),
            P("req", "cuts", None),
            P("req", "cuts", None),
            P("req", "cuts", None),
            P("req", "cuts", None),
            P("req"),
            P(),
            P("req", "cuts", None),
            P(),
            P(),
            P(),
            P("req", "cuts", None),
            P("req", None, "cuts"),
            P("req", None, "cuts"),
            P("req", None, "cuts"),
        ),
        out_specs=P("req", "cuts", None),
        check_vma=False,
    )
```

```python
from functools import partial

import jax
import jax.numpy as jnp
import numpy as np
from jax import lax
from jax.sharding import PartitionSpec as P
from jax.experimental import pallas as pl
from jax.experimental.pallas import tpu as pltpu

MAXDIST = 128


def shortened(value):
    return jax.tree.map(lambda a: a.astype(jnp.bfloat16) if a.dtype == jnp.float32 else a, value)


def bucket_number(distance, bucket_count, reach_limit):
    exact_count = bucket_count // 2
    if distance < exact_count:
        return distance
    level_value = exact_count + int(
        np.floor(exact_count * np.log(distance / exact_count) / np.log(reach_limit / exact_count))
    )
    return min(bucket_count - 1, level_value)


def bucket_edges(bucket_count, reach_limit):
    edge_list = []
    for target in range(1, bucket_count):
        probe_value = 0
        while bucket_number(probe_value, bucket_count, reach_limit) < target:
            probe_value += 1
        edge_list.append(probe_value)
    return edge_list


def bucket_index(distance, edge_list):
    bucket_level = jnp.zeros(distance.shape, jnp.int32)
    for edge_value in edge_list:
        bucket_level = bucket_level + (distance >= edge_value).astype(jnp.int32)
    return bucket_level


def attention_kernel(scalars, q_ref, k_ref, v_ref, tc_ref, tn_ref, live_ref, o_ref):
    q_rows = q_ref.shape[0]
    key_blocks, key_span, head_dim = k_ref.shape
    cache_rows = tc_ref.shape[2] - q_rows
    new_rows = key_span - cache_rows
    cache_width = tc_ref.shape[2]
    new_width = tn_ref.shape[2]
    query = q_ref[...]

    def one_block(g, carry):
        best, weighted, factor_sum = carry
        scores = lax.dot_general(
            query, k_ref[g], (((1,), (1,)), ((), ())), preferred_element_type=jnp.float32
        )
        cache_table = jnp.broadcast_to(tc_ref[0, pl.ds(g, 1), :], (q_rows, cache_width))
        cache_bias = pltpu.roll(cache_table, cache_width - q_rows, 1, stride=1, stride_axis=0)
        new_table = jnp.broadcast_to(tn_ref[0, pl.ds(g, 1), :], (q_rows, new_width))
        new_bias = pltpu.roll(new_table, new_width - q_rows, 1, stride=1, stride_axis=0)
        bias = jnp.concatenate(
            [cache_bias[:, :cache_rows] + live_ref[pl.ds(g, 1), :], new_bias[:, :new_rows]], axis=1
        )
        masked = scores + bias
        peak = jnp.max(masked, axis=1, keepdims=True)
        weights = jnp.exp(masked - peak)
        total = jnp.sum(weights, axis=1, keepdims=True)
        numerator = jnp.dot(
            weights.astype(jnp.bfloat16), v_ref[g], preferred_element_type=jnp.float32
        )
        block_out = (numerator / jnp.maximum(total, 1.0)).astype(jnp.bfloat16).astype(jnp.float32)
        new_best = jnp.maximum(best, peak)
        rescale = jnp.exp(best - new_best)
        factor = jnp.exp(peak - new_best) * total
        return (new_best, weighted * rescale + factor * block_out, factor_sum * rescale + factor)

    start = (
        jnp.full((q_rows, 1), -1e30, jnp.float32),
        jnp.zeros((q_rows, head_dim), jnp.float32),
        jnp.zeros((q_rows, 1), jnp.float32),
    )
    best, weighted, factor_sum = lax.fori_loop(0, key_blocks, one_block, start)
    o_ref[...] = (weighted / factor_sum).astype(o_ref.dtype)


def bias_tables(head_table, length, q_rows, cache_rows, new_rows, query_blocks, key_blocks):
    edges = bucket_edges(head_table.shape[1], MAXDIST)
    blocks = jnp.arange(query_blocks, dtype=jnp.int32)[:, None, None]
    key_ids = jnp.arange(key_blocks, dtype=jnp.int32)[None, :, None]
    cache_lanes = jnp.arange(cache_rows + q_rows, dtype=jnp.int32)[None, None, :]
    new_lanes = jnp.arange(new_rows + q_rows, dtype=jnp.int32)[None, None, :]
    cache_distance = length + blocks * q_rows - key_ids * cache_rows + q_rows - cache_lanes
    new_distance = (blocks * q_rows - key_ids * new_rows) + q_rows - new_lanes
    cache_bucket = bucket_index(jnp.maximum(cache_distance, 0), edges)
    new_bucket = bucket_index(jnp.maximum(new_distance, 0), edges)
    choices = jnp.arange(head_table.shape[1], dtype=jnp.int32)
    cache_hot = (cache_bucket[..., None] == choices).astype(jnp.float32)
    new_hot = (new_bucket[..., None] == choices).astype(jnp.float32)
    cache_table = jnp.einsum("agmk,hk->agm", cache_hot, head_table, precision=lax.Precision.HIGHEST)
    new_table = jnp.einsum("agmk,hk->agm", new_hot, head_table, precision=lax.Precision.HIGHEST)
    new_table = jnp.where(new_distance >= 0, new_table, -1e30)
    cache_slots = key_ids[0] * cache_rows + jnp.arange(cache_rows, dtype=jnp.int32)[None, :]
    live = jnp.where(cache_slots < length, 0.0, -1e30).astype(jnp.float32)
    return cache_table, new_table, live


def block_partials(query_rows, key_rows, value_rows, head_table, length, cache_rows, q_rows):
    key_blocks, key_span, head_dim = key_rows.shape
    new_rows = key_span - cache_rows
    query_total = query_rows.shape[0]
    query_blocks = query_total // q_rows
    cache_table, new_table, live = bias_tables(
        head_table, length, q_rows, cache_rows, new_rows, query_blocks, key_blocks
    )
    scalars = jnp.stack([length]).astype(jnp.int32)
    grid_spec = pltpu.PrefetchScalarGridSpec(
        num_scalar_prefetch=1,
        grid=(query_blocks,),
        in_specs=[
            pl.BlockSpec((q_rows, head_dim), lambda b, s: (b, 0)),
            pl.BlockSpec((key_blocks, key_span, head_dim), lambda b, s: (0, 0, 0)),
            pl.BlockSpec((key_blocks, key_span, head_dim), lambda b, s: (0, 0, 0)),
            pl.BlockSpec((1, key_blocks, cache_table.shape[2]), lambda b, s: (b, 0, 0)),
            pl.BlockSpec((1, key_blocks, new_table.shape[2]), lambda b, s: (b, 0, 0)),
            pl.BlockSpec(live.shape, lambda b, s: (0, 0)),
        ],
        out_specs=pl.BlockSpec((q_rows, head_dim), lambda b, s: (b, 0)),
    )
    pairs = query_total * key_span * key_blocks
    return pl.pallas_call(
        attention_kernel,
        grid_spec=grid_spec,
        out_shape=jax.ShapeDtypeStruct((query_total, head_dim), jnp.bfloat16),
        cost_estimate=pl.CostEstimate(
            flops=4 * pairs * head_dim,
            transcendentals=pairs,
            bytes_accessed=4 * query_total * head_dim * key_blocks + 4 * key_span * key_blocks * head_dim,
        ),
    )(scalars, query_rows, key_rows, value_rows, cache_table, new_table, live)


def per_device(
    queries,
    new_keys,
    new_values,
    cache_keys,
    cache_values,
    cache_lengths,
    relative_bias,
    residual,
    out_weight,
    norm_gain,
    router_weight,
    routes,
    gate_weight,
    up_weight,
    down_weight,
):
    cut_count = lax.axis_size("cuts")
    cut_index = lax.axis_index("cuts")
    q_rows = queries.shape[1]
    cache_rows = cache_keys.shape[1]
    model_width = queries.shape[2]
    head_count = relative_bias.shape[0]
    head_dim = model_width // head_count
    bucket_count = relative_bias.shape[1]
    length = cache_lengths[0]
    query_total = q_rows * cut_count
    local_keys = jnp.concatenate([cache_keys[0], new_keys[0]], axis=0)
    local_values = jnp.concatenate([cache_values[0], new_values[0]], axis=0)
    key_span = local_keys.shape[0]
    packed = jnp.concatenate(
        [queries[0] * jnp.asarray(0.125, queries.dtype), local_keys, local_values], axis=0
    )
    packed = lax.all_to_all(
        packed.reshape(packed.shape[0], head_count, head_dim), "cuts", split_axis=1, concat_axis=0, tiled=True
    ).reshape(cut_count, packed.shape[0], head_dim)
    head_queries = packed[:, :q_rows].reshape(query_total, head_dim)
    head_keys = packed[:, q_rows:q_rows + key_span]
    head_values = packed[:, q_rows + key_span:]
    head_table = lax.dynamic_slice_in_dim(relative_bias, cut_index, 1, 0)
    head_out = block_partials(
        head_queries, head_keys, head_values, head_table, length, cache_rows, q_rows
    )
    attended = lax.all_to_all(
        head_out.reshape(cut_count, q_rows, head_dim), "cuts", split_axis=0, concat_axis=0, tiled=True
    ).transpose(1, 0, 2).reshape(q_rows, model_width)
    hidden = residual[0].astype(jnp.float32) + jnp.dot(
        attended, out_weight, preferred_element_type=jnp.float32
    )
    inv_rms = lax.rsqrt(jnp.mean(hidden * hidden, axis=1, keepdims=True) + 1e-06)
    normed = (hidden * inv_rms * norm_gain.astype(jnp.float32)).astype(jnp.bfloat16)
    experts = router_weight.shape[1]
    capacity = (10 * q_rows + 4 * experts - 1) // (4 * experts)
    logits = jnp.dot(normed, router_weight, preferred_element_type=jnp.float32)
    chosen = routes[0]
    onehot = (chosen[:, :, None] == jnp.arange(experts, dtype=jnp.int32)[None, None, :]).astype(
        jnp.float32
    )
    gate_values = jax.nn.sigmoid(jnp.sum(onehot * logits[:, None, :], axis=2))
    named_count = jnp.sum(onehot, axis=1)
    earlier_mask = (jnp.arange(q_rows)[:, None] > jnp.arange(q_rows)[None, :]).astype(jnp.bfloat16)
    earlier = jnp.dot(
        earlier_mask, named_count.astype(jnp.bfloat16), preferred_element_type=jnp.float32
    )
    slot_number = jnp.sum(onehot * earlier[:, None, :], axis=2)
    slot_hot = (
        slot_number[:, :, None] == jnp.arange(capacity, dtype=jnp.float32)[None, None, :]
    ).astype(jnp.float32)
    dispatch = jnp.einsum("tke,tkc->ect", onehot, slot_hot)
    buffers = jnp.einsum(
        "ect,td->ecd", dispatch.astype(jnp.bfloat16), normed, preferred_element_type=jnp.float32
    ).astype(jnp.bfloat16)
    arrived = lax.all_to_all(buffers, "req", split_axis=0, concat_axis=0, tiled=True)
    full_gate = lax.all_gather(gate_weight[0], "cuts", axis=1, tiled=True)
    full_up = lax.all_gather(up_weight[0], "cuts", axis=1, tiled=True)
    full_down = lax.all_gather(down_weight[0], "cuts", axis=1, tiled=True)
    flat_rows = arrived.reshape(-1, model_width)
    gate_act = jnp.dot(flat_rows, full_gate, preferred_element_type=jnp.float32)
    up_act = jnp.dot(flat_rows, full_up, preferred_element_type=jnp.float32)
    act_rows = (jax.nn.gelu(gate_act) * up_act).astype(jnp.bfloat16)
    expert_out = lax.dot_general(
        act_rows, full_down, (((1,), (1,)), ((), ())), preferred_element_type=jnp.float32
    ).astype(jnp.bfloat16).reshape(arrived.shape)
    returned = lax.all_to_all(expert_out, "req", split_axis=0, concat_axis=0, tiled=True)
    combine = jnp.einsum(
        "tke,tkc,tk->ect", onehot, slot_hot, gate_values, precision=lax.Precision.HIGHEST
    )
    gathered_back = jnp.einsum(
        "ect,ecd->td", combine, returned.astype(jnp.float32), precision=lax.Precision.HIGHEST
    )
    layer_out = hidden + gathered_back
    return layer_out.astype(jnp.bfloat16)[None]


def solution(mesh):
    return jax.shard_map(
        per_device,
        mesh=mesh,
        in_specs=(
            P("req", "cuts", None),
            P("req", "cuts", None),
            P("req", "cuts", None),
            P("req", "cuts", None),
            P("req", "cuts", None),
            P("req"),
            P(),
            P("req", "cuts", None),
            P(),
            P(),
            P(),
            P("req", "cuts", None),
            P("req", None, "cuts"),
            P("req", None, "cuts"),
            P("req", None, "cuts"),
        ),
        out_specs=P("req", "cuts", None),
        check_vma=False,
    )
```

```python
from functools import partial

import jax
import jax.numpy as jnp
import numpy as np
from jax import lax
from jax.sharding import PartitionSpec as P
from jax.experimental import pallas as pl
from jax.experimental.pallas import tpu as pltpu

MAXDIST = 128


def shortened(value):
    return jax.tree.map(lambda a: a.astype(jnp.bfloat16) if a.dtype == jnp.float32 else a, value)


def bucket_number(distance, bucket_count, reach_limit):
    exact_count = bucket_count // 2
    if distance < exact_count:
        return distance
    level_value = exact_count + int(
        np.floor(exact_count * np.log(distance / exact_count) / np.log(reach_limit / exact_count))
    )
    return min(bucket_count - 1, level_value)


def bucket_edges(bucket_count, reach_limit):
    edge_list = []
    for target in range(1, bucket_count):
        probe_value = 0
        while bucket_number(probe_value, bucket_count, reach_limit) < target:
            probe_value += 1
        edge_list.append(probe_value)
    return edge_list


def bucket_index(distance, edge_list):
    bucket_level = jnp.zeros(distance.shape, jnp.int32)
    for edge_value in edge_list:
        bucket_level = bucket_level + (distance >= edge_value).astype(jnp.int32)
    return bucket_level


def attention_kernel(scalars, q_ref, k_ref, v_ref, tc_ref, tn_ref, live_ref, o_ref):
    q_rows = q_ref.shape[0]
    key_blocks, key_span, head_dim = k_ref.shape
    cache_rows = tc_ref.shape[2] - q_rows
    new_rows = key_span - cache_rows
    cache_width = tc_ref.shape[2]
    new_width = tn_ref.shape[2]
    query = q_ref[...]

    def one_block(g, carry):
        best, weighted, factor_sum = carry
        scores = lax.dot_general(
            query, k_ref[g], (((1,), (1,)), ((), ())), preferred_element_type=jnp.float32
        )
        cache_table = jnp.broadcast_to(tc_ref[0, pl.ds(g, 1), :], (q_rows, cache_width))
        cache_bias = pltpu.roll(cache_table, cache_width - q_rows, 1, stride=1, stride_axis=0)
        new_table = jnp.broadcast_to(tn_ref[0, pl.ds(g, 1), :], (q_rows, new_width))
        new_bias = pltpu.roll(new_table, new_width - q_rows, 1, stride=1, stride_axis=0)
        bias = jnp.concatenate(
            [cache_bias[:, :cache_rows] + live_ref[pl.ds(g, 1), :], new_bias[:, :new_rows]], axis=1
        )
        masked = scores + bias
        peak = jnp.max(masked, axis=1, keepdims=True)
        weights = jnp.exp(masked - peak)
        total = jnp.sum(weights, axis=1, keepdims=True)
        numerator = jnp.dot(
            weights.astype(jnp.bfloat16), v_ref[g], preferred_element_type=jnp.float32
        )
        block_out = (numerator / jnp.maximum(total, 1.0)).astype(jnp.bfloat16).astype(jnp.float32)
        new_best = jnp.maximum(best, peak)
        rescale = jnp.exp(best - new_best)
        factor = jnp.exp(peak - new_best) * total
        return (new_best, weighted * rescale + factor * block_out, factor_sum * rescale + factor)

    start = (
        jnp.full((q_rows, 1), -1e30, jnp.float32),
        jnp.zeros((q_rows, head_dim), jnp.float32),
        jnp.zeros((q_rows, 1), jnp.float32),
    )
    best, weighted, factor_sum = lax.fori_loop(0, key_blocks, one_block, start, unroll=2)
    o_ref[...] = (weighted / factor_sum).astype(o_ref.dtype)


def bias_tables(head_table, length, q_rows, cache_rows, new_rows, query_blocks, key_blocks):
    edges = bucket_edges(head_table.shape[1], MAXDIST)
    blocks = jnp.arange(query_blocks, dtype=jnp.int32)[:, None, None]
    key_ids = jnp.arange(key_blocks, dtype=jnp.int32)[None, :, None]
    cache_lanes = jnp.arange(cache_rows + q_rows, dtype=jnp.int32)[None, None, :]
    new_lanes = jnp.arange(new_rows + q_rows, dtype=jnp.int32)[None, None, :]
    cache_distance = length + blocks * q_rows - key_ids * cache_rows + q_rows - cache_lanes
    new_distance = (blocks * q_rows - key_ids * new_rows) + q_rows - new_lanes
    cache_bucket = bucket_index(jnp.maximum(cache_distance, 0), edges)
    new_bucket = bucket_index(jnp.maximum(new_distance, 0), edges)
    choices = jnp.arange(head_table.shape[1], dtype=jnp.int32)
    cache_hot = (cache_bucket[..., None] == choices).astype(jnp.float32)
    new_hot = (new_bucket[..., None] == choices).astype(jnp.float32)
    cache_table = jnp.einsum("agmk,hk->agm", cache_hot, head_table, precision=lax.Precision.HIGHEST)
    new_table = jnp.einsum("agmk,hk->agm", new_hot, head_table, precision=lax.Precision.HIGHEST)
    new_table = jnp.where(new_distance >= 0, new_table, -1e30)
    cache_slots = key_ids[0] * cache_rows + jnp.arange(cache_rows, dtype=jnp.int32)[None, :]
    live = jnp.where(cache_slots < length, 0.0, -1e30).astype(jnp.float32)
    return cache_table, new_table, live


def block_partials(query_rows, key_rows, value_rows, head_table, length, cache_rows, q_rows):
    q_rows = 2 * q_rows
    key_blocks, key_span, head_dim = key_rows.shape
    new_rows = key_span - cache_rows
    query_total = query_rows.shape[0]
    query_blocks = query_total // q_rows
    cache_table, new_table, live = bias_tables(
        head_table, length, q_rows, cache_rows, new_rows, query_blocks, key_blocks
    )
    scalars = jnp.stack([length]).astype(jnp.int32)
    grid_spec = pltpu.PrefetchScalarGridSpec(
        num_scalar_prefetch=1,
        grid=(query_blocks,),
        in_specs=[
            pl.BlockSpec((q_rows, head_dim), lambda b, s: (b, 0)),
            pl.BlockSpec((key_blocks, key_span, head_dim), lambda b, s: (0, 0, 0)),
            pl.BlockSpec((key_blocks, key_span, head_dim), lambda b, s: (0, 0, 0)),
            pl.BlockSpec((1, key_blocks, cache_table.shape[2]), lambda b, s: (b, 0, 0)),
            pl.BlockSpec((1, key_blocks, new_table.shape[2]), lambda b, s: (b, 0, 0)),
            pl.BlockSpec(live.shape, lambda b, s: (0, 0)),
        ],
        out_specs=pl.BlockSpec((q_rows, head_dim), lambda b, s: (b, 0)),
    )
    pairs = query_total * key_span * key_blocks
    return pl.pallas_call(
        attention_kernel,
        grid_spec=grid_spec,
        out_shape=jax.ShapeDtypeStruct((query_total, head_dim), jnp.bfloat16),
        cost_estimate=pl.CostEstimate(
            flops=4 * pairs * head_dim,
            transcendentals=pairs,
            bytes_accessed=4 * query_total * head_dim * key_blocks + 4 * key_span * key_blocks * head_dim,
        ),
    )(scalars, query_rows, key_rows, value_rows, cache_table, new_table, live)


def per_device(
    queries,
    new_keys,
    new_values,
    cache_keys,
    cache_values,
    cache_lengths,
    relative_bias,
    residual,
    out_weight,
    norm_gain,
    router_weight,
    routes,
    gate_weight,
    up_weight,
    down_weight,
):
    cut_count = lax.axis_size("cuts")
    cut_index = lax.axis_index("cuts")
    q_rows = queries.shape[1]
    cache_rows = cache_keys.shape[1]
    model_width = queries.shape[2]
    head_count = relative_bias.shape[0]
    head_dim = model_width // head_count
    bucket_count = relative_bias.shape[1]
    length = cache_lengths[0]
    query_total = q_rows * cut_count
    local_keys = jnp.concatenate([cache_keys[0], new_keys[0]], axis=0)
    local_values = jnp.concatenate([cache_values[0], new_values[0]], axis=0)
    key_span = local_keys.shape[0]
    packed = jnp.concatenate(
        [queries[0] * jnp.asarray(0.125, queries.dtype), local_keys, local_values], axis=0
    )
    packed = lax.all_to_all(
        packed.reshape(packed.shape[0], head_count, head_dim), "cuts", split_axis=1, concat_axis=0, tiled=True
    ).reshape(cut_count, packed.shape[0], head_dim)
    head_queries = packed[:, :q_rows].reshape(query_total, head_dim)
    head_keys = packed[:, q_rows:q_rows + key_span]
    head_values = packed[:, q_rows + key_span:]
    head_table = lax.dynamic_slice_in_dim(relative_bias, cut_index, 1, 0)
    head_out = block_partials(
        head_queries, head_keys, head_values, head_table, length, cache_rows, q_rows
    )
    attended = lax.all_to_all(
        head_out.reshape(cut_count, q_rows, head_dim), "cuts", split_axis=0, concat_axis=0, tiled=True
    ).transpose(1, 0, 2).reshape(q_rows, model_width)
    hidden = residual[0].astype(jnp.float32) + jnp.dot(
        attended, out_weight, preferred_element_type=jnp.float32
    )
    inv_rms = lax.rsqrt(jnp.mean(hidden * hidden, axis=1, keepdims=True) + 1e-06)
    normed = (hidden * inv_rms * norm_gain.astype(jnp.float32)).astype(jnp.bfloat16)
    experts = router_weight.shape[1]
    capacity = (10 * q_rows + 4 * experts - 1) // (4 * experts)
    logits = jnp.dot(normed, router_weight, preferred_element_type=jnp.float32)
    chosen = routes[0]
    onehot = (chosen[:, :, None] == jnp.arange(experts, dtype=jnp.int32)[None, None, :]).astype(
        jnp.float32
    )
    gate_values = jax.nn.sigmoid(jnp.sum(onehot * logits[:, None, :], axis=2))
    named_count = jnp.sum(onehot, axis=1)
    earlier_mask = (jnp.arange(q_rows)[:, None] > jnp.arange(q_rows)[None, :]).astype(jnp.bfloat16)
    earlier = jnp.dot(
        earlier_mask, named_count.astype(jnp.bfloat16), preferred_element_type=jnp.float32
    )
    slot_number = jnp.sum(onehot * earlier[:, None, :], axis=2)
    slot_hot = (
        slot_number[:, :, None] == jnp.arange(capacity, dtype=jnp.float32)[None, None, :]
    ).astype(jnp.float32)
    dispatch = jnp.einsum("tke,tkc->ect", onehot, slot_hot)
    buffers = jnp.einsum(
        "ect,td->ecd", dispatch.astype(jnp.bfloat16), normed, preferred_element_type=jnp.float32
    ).astype(jnp.bfloat16)
    arrived = lax.all_to_all(buffers, "req", split_axis=0, concat_axis=0, tiled=True)
    full_gate = lax.all_gather(gate_weight[0], "cuts", axis=1, tiled=True)
    full_up = lax.all_gather(up_weight[0], "cuts", axis=1, tiled=True)
    full_down = lax.all_gather(down_weight[0], "cuts", axis=1, tiled=True)
    flat_rows = arrived.reshape(-1, model_width)
    gate_act = jnp.dot(flat_rows, full_gate, preferred_element_type=jnp.float32)
    up_act = jnp.dot(flat_rows, full_up, preferred_element_type=jnp.float32)
    act_rows = (jax.nn.gelu(gate_act) * up_act).astype(jnp.bfloat16)
    expert_out = lax.dot_general(
        act_rows, full_down, (((1,), (1,)), ((), ())), preferred_element_type=jnp.float32
    ).astype(jnp.bfloat16).reshape(arrived.shape)
    returned = lax.all_to_all(expert_out, "req", split_axis=0, concat_axis=0, tiled=True)
    combine = jnp.einsum(
        "tke,tkc,tk->ect", onehot, slot_hot, gate_values, precision=lax.Precision.HIGHEST
    )
    gathered_back = jnp.einsum(
        "ect,ecd->td", combine, returned.astype(jnp.float32), precision=lax.Precision.HIGHEST
    )
    layer_out = hidden + gathered_back
    return layer_out.astype(jnp.bfloat16)[None]


def solution(mesh):
    return jax.shard_map(
        per_device,
        mesh=mesh,
        in_specs=(
            P("req", "cuts", None),
            P("req", "cuts", None),
            P("req", "cuts", None),
            P("req", "cuts", None),
            P("req", "cuts", None),
            P("req"),
            P(),
            P("req", "cuts", None),
            P(),
            P(),
            P(),
            P("req", "cuts", None),
            P("req", None, "cuts"),
            P("req", None, "cuts"),
            P("req", None, "cuts"),
        ),
        out_specs=P("req", "cuts", None),
        check_vma=False,
    )
```

```python
from functools import partial

import jax
import jax.numpy as jnp
import numpy as np
from jax import lax
from jax.sharding import PartitionSpec as P
from jax.experimental import pallas as pl
from jax.experimental.pallas import tpu as pltpu

MAXDIST = 128


def shortened(value):
    return jax.tree.map(lambda a: a.astype(jnp.bfloat16) if a.dtype == jnp.float32 else a, value)


def bucket_number(distance, bucket_count, reach_limit):
    exact_count = bucket_count // 2
    if distance < exact_count:
        return distance
    level_value = exact_count + int(
        np.floor(exact_count * np.log(distance / exact_count) / np.log(reach_limit / exact_count))
    )
    return min(bucket_count - 1, level_value)


def bucket_edges(bucket_count, reach_limit):
    edge_list = []
    for target in range(1, bucket_count):
        probe_value = 0
        while bucket_number(probe_value, bucket_count, reach_limit) < target:
            probe_value += 1
        edge_list.append(probe_value)
    return edge_list


def bucket_index(distance, edge_list):
    bucket_level = jnp.zeros(distance.shape, jnp.int32)
    for edge_value in edge_list:
        bucket_level = bucket_level + (distance >= edge_value).astype(jnp.int32)
    return bucket_level


def attention_kernel(scalars, q_ref, k_ref, v_ref, tc_ref, tn_ref, live_ref, o_ref):
    key_blocks, key_span, head_dim = k_ref.shape
    q_rows = q_ref.shape[0] * q_ref.shape[1]
    cache_rows = tc_ref.shape[2] - q_rows
    new_rows = key_span - cache_rows
    cache_width = tc_ref.shape[2]
    new_width = tn_ref.shape[2]
    query = q_ref[...].reshape(q_rows, head_dim)

    def one_block(g, carry):
        best, weighted, factor_sum = carry
        scores = lax.dot_general(
            query, k_ref[g], (((1,), (1,)), ((), ())), preferred_element_type=jnp.float32
        )
        cache_table = jnp.broadcast_to(tc_ref[0, pl.ds(g, 1), :], (q_rows, cache_width))
        cache_bias = pltpu.roll(cache_table, cache_width - q_rows, 1, stride=1, stride_axis=0)
        new_table = jnp.broadcast_to(tn_ref[0, pl.ds(g, 1), :], (q_rows, new_width))
        new_bias = pltpu.roll(new_table, new_width - q_rows, 1, stride=1, stride_axis=0)
        bias = jnp.concatenate(
            [cache_bias[:, :cache_rows] + live_ref[pl.ds(g, 1), :], new_bias[:, :new_rows]], axis=1
        )
        masked = scores + bias
        peak = jnp.max(masked, axis=1, keepdims=True)
        weights = jnp.exp(masked - peak)
        total = jnp.sum(weights, axis=1, keepdims=True)
        numerator = jnp.dot(
            weights.astype(jnp.bfloat16), v_ref[g], preferred_element_type=jnp.float32
        )
        block_out = (numerator / jnp.maximum(total, 1.0)).astype(jnp.bfloat16).astype(jnp.float32)
        new_best = jnp.maximum(best, peak)
        rescale = jnp.exp(best - new_best)
        factor = jnp.exp(peak - new_best) * total
        return (new_best, weighted * rescale + factor * block_out, factor_sum * rescale + factor)

    start = (
        jnp.full((q_rows, 1), -1e30, jnp.float32),
        jnp.zeros((q_rows, head_dim), jnp.float32),
        jnp.zeros((q_rows, 1), jnp.float32),
    )
    best, weighted, factor_sum = lax.fori_loop(0, key_blocks, one_block, start, unroll=2)
    o_ref[...] = (weighted / factor_sum).astype(o_ref.dtype)


def bias_tables(head_table, length, q_rows, cache_rows, new_rows, query_blocks, key_blocks):
    edges = bucket_edges(head_table.shape[1], MAXDIST)
    blocks = jnp.arange(query_blocks, dtype=jnp.int32)[:, None, None]
    key_ids = jnp.arange(key_blocks, dtype=jnp.int32)[None, :, None]
    cache_lanes = jnp.arange(cache_rows + q_rows, dtype=jnp.int32)[None, None, :]
    new_lanes = jnp.arange(new_rows + q_rows, dtype=jnp.int32)[None, None, :]
    cache_distance = length + blocks * q_rows - key_ids * cache_rows + q_rows - cache_lanes
    new_distance = (blocks * q_rows - key_ids * new_rows) + q_rows - new_lanes
    cache_bucket = bucket_index(jnp.maximum(cache_distance, 0), edges)
    new_bucket = bucket_index(jnp.maximum(new_distance, 0), edges)
    choices = jnp.arange(head_table.shape[1], dtype=jnp.int32)
    cache_hot = (cache_bucket[..., None] == choices).astype(jnp.float32)
    new_hot = (new_bucket[..., None] == choices).astype(jnp.float32)
    cache_table = jnp.einsum("agmk,hk->agm", cache_hot, head_table, precision=lax.Precision.HIGHEST)
    new_table = jnp.einsum("agmk,hk->agm", new_hot, head_table, precision=lax.Precision.HIGHEST)
    new_table = jnp.where(new_distance >= 0, new_table, -1e30)
    cache_slots = key_ids[0] * cache_rows + jnp.arange(cache_rows, dtype=jnp.int32)[None, :]
    live = jnp.where(cache_slots < length, 0.0, -1e30).astype(jnp.float32)
    return cache_table, new_table, live


def block_partials(packed, head_table, length, cache_rows, q_rows):
    source_rows = q_rows
    q_rows = 2 * q_rows
    key_blocks, packed_rows, head_dim = packed.shape
    key_span = (packed_rows - source_rows) // 2
    new_rows = key_span - cache_rows
    query_total = key_blocks * source_rows
    query_blocks = query_total // q_rows
    sources = q_rows // source_rows
    query_offset = 2 * key_span // source_rows
    cache_table, new_table, live = bias_tables(
        head_table, length, q_rows, cache_rows, new_rows, query_blocks, key_blocks
    )
    scalars = jnp.stack([length]).astype(jnp.int32)
    grid_spec = pltpu.PrefetchScalarGridSpec(
        num_scalar_prefetch=1,
        grid=(query_blocks,),
        in_specs=[
            pl.BlockSpec((sources, source_rows, head_dim), lambda b, s: (b, query_offset, 0)),
            pl.BlockSpec((key_blocks, key_span, head_dim), lambda b, s: (0, 0, 0)),
            pl.BlockSpec((key_blocks, key_span, head_dim), lambda b, s: (0, 1, 0)),
            pl.BlockSpec((1, key_blocks, cache_table.shape[2]), lambda b, s: (b, 0, 0)),
            pl.BlockSpec((1, key_blocks, new_table.shape[2]), lambda b, s: (b, 0, 0)),
            pl.BlockSpec(live.shape, lambda b, s: (0, 0)),
        ],
        out_specs=pl.BlockSpec((q_rows, head_dim), lambda b, s: (b, 0)),
    )
    pairs = query_total * key_span * key_blocks
    return pl.pallas_call(
        attention_kernel,
        grid_spec=grid_spec,
        out_shape=jax.ShapeDtypeStruct((query_total, head_dim), jnp.bfloat16),
        cost_estimate=pl.CostEstimate(
            flops=4 * pairs * head_dim,
            transcendentals=pairs,
            bytes_accessed=4 * query_total * head_dim * key_blocks + 4 * key_span * key_blocks * head_dim,
        ),
    )(scalars, packed, packed, packed, cache_table, new_table, live)


def per_device(
    queries,
    new_keys,
    new_values,
    cache_keys,
    cache_values,
    cache_lengths,
    relative_bias,
    residual,
    out_weight,
    norm_gain,
    router_weight,
    routes,
    gate_weight,
    up_weight,
    down_weight,
):
    cut_count = lax.axis_size("cuts")
    cut_index = lax.axis_index("cuts")
    q_rows = queries.shape[1]
    cache_rows = cache_keys.shape[1]
    model_width = queries.shape[2]
    head_count = relative_bias.shape[0]
    head_dim = model_width // head_count
    bucket_count = relative_bias.shape[1]
    length = cache_lengths[0]
    query_total = q_rows * cut_count
    local_keys = jnp.concatenate([cache_keys[0], new_keys[0]], axis=0)
    local_values = jnp.concatenate([cache_values[0], new_values[0]], axis=0)
    key_span = local_keys.shape[0]
    packed = jnp.concatenate(
        [local_keys, local_values, queries[0] * jnp.asarray(0.125, queries.dtype)], axis=0
    )
    packed = lax.all_to_all(
        packed.reshape(packed.shape[0], head_count, head_dim), "cuts", split_axis=1, concat_axis=0, tiled=True
    ).reshape(cut_count, packed.shape[0], head_dim)
    head_table = lax.dynamic_slice_in_dim(relative_bias, cut_index, 1, 0)
    head_out = block_partials(packed, head_table, length, cache_rows, q_rows)
    attended = lax.all_to_all(
        head_out.reshape(cut_count, q_rows, head_dim), "cuts", split_axis=0, concat_axis=0, tiled=True
    ).transpose(1, 0, 2).reshape(q_rows, model_width)
    hidden = residual[0].astype(jnp.float32) + jnp.dot(
        attended, out_weight, preferred_element_type=jnp.float32
    )
    inv_rms = lax.rsqrt(jnp.mean(hidden * hidden, axis=1, keepdims=True) + 1e-06)
    normed = (hidden * inv_rms * norm_gain.astype(jnp.float32)).astype(jnp.bfloat16)
    experts = router_weight.shape[1]
    capacity = (10 * q_rows + 4 * experts - 1) // (4 * experts)
    logits = jnp.dot(normed, router_weight, preferred_element_type=jnp.float32)
    chosen = routes[0]
    onehot = (chosen[:, :, None] == jnp.arange(experts, dtype=jnp.int32)[None, None, :]).astype(
        jnp.float32
    )
    gate_values = jax.nn.sigmoid(jnp.sum(onehot * logits[:, None, :], axis=2))
    named_count = jnp.sum(onehot, axis=1)
    earlier_mask = (jnp.arange(q_rows)[:, None] > jnp.arange(q_rows)[None, :]).astype(jnp.bfloat16)
    earlier = jnp.dot(
        earlier_mask, named_count.astype(jnp.bfloat16), preferred_element_type=jnp.float32
    )
    slot_number = jnp.sum(onehot * earlier[:, None, :], axis=2)
    slot_hot = (
        slot_number[:, :, None] == jnp.arange(capacity, dtype=jnp.float32)[None, None, :]
    ).astype(jnp.float32)
    dispatch = jnp.einsum("tke,tkc->ect", onehot, slot_hot)
    buffers = jnp.einsum(
        "ect,td->ecd", dispatch.astype(jnp.bfloat16), normed, preferred_element_type=jnp.float32
    ).astype(jnp.bfloat16)
    arrived = lax.all_to_all(buffers, "req", split_axis=0, concat_axis=0, tiled=True)
    full_gate = lax.all_gather(gate_weight[0], "cuts", axis=1, tiled=True)
    full_up = lax.all_gather(up_weight[0], "cuts", axis=1, tiled=True)
    full_down = lax.all_gather(down_weight[0], "cuts", axis=1, tiled=True)
    flat_rows = arrived.reshape(-1, model_width)
    gate_act = jnp.dot(flat_rows, full_gate, preferred_element_type=jnp.float32)
    up_act = jnp.dot(flat_rows, full_up, preferred_element_type=jnp.float32)
    act_rows = (jax.nn.gelu(gate_act) * up_act).astype(jnp.bfloat16)
    expert_out = lax.dot_general(
        act_rows, full_down, (((1,), (1,)), ((), ())), preferred_element_type=jnp.float32
    ).astype(jnp.bfloat16).reshape(arrived.shape)
    returned = lax.all_to_all(expert_out, "req", split_axis=0, concat_axis=0, tiled=True)
    combine = jnp.einsum(
        "tke,tkc,tk->ect", onehot, slot_hot, gate_values, precision=lax.Precision.HIGHEST
    )
    gathered_back = jnp.einsum(
        "ect,ecd->td", combine, returned.astype(jnp.float32), precision=lax.Precision.HIGHEST
    )
    layer_out = hidden + gathered_back
    return layer_out.astype(jnp.bfloat16)[None]


def solution(mesh):
    return jax.shard_map(
        per_device,
        mesh=mesh,
        in_specs=(
            P("req", "cuts", None),
            P("req", "cuts", None),
            P("req", "cuts", None),
            P("req", "cuts", None),
            P("req", "cuts", None),
            P("req"),
            P(),
            P("req", "cuts", None),
            P(),
            P(),
            P(),
            P("req", "cuts", None),
            P("req", None, "cuts"),
            P("req", None, "cuts"),
            P("req", None, "cuts"),
        ),
        out_specs=P("req", "cuts", None),
        check_vma=False,
    )
```

```python
from functools import partial

import jax
import jax.numpy as jnp
import numpy as np
from jax import lax
from jax.sharding import PartitionSpec as P
from jax.experimental import pallas as pl
from jax.experimental.pallas import tpu as pltpu

MAXDIST = 128


def shortened(value):
    return jax.tree.map(lambda a: a.astype(jnp.bfloat16) if a.dtype == jnp.float32 else a, value)


def bucket_number(distance, bucket_count, reach_limit):
    exact_count = bucket_count // 2
    if distance < exact_count:
        return distance
    level_value = exact_count + int(
        np.floor(exact_count * np.log(distance / exact_count) / np.log(reach_limit / exact_count))
    )
    return min(bucket_count - 1, level_value)


def bucket_edges(bucket_count, reach_limit):
    edge_list = []
    for target in range(1, bucket_count):
        probe_value = 0
        while bucket_number(probe_value, bucket_count, reach_limit) < target:
            probe_value += 1
        edge_list.append(probe_value)
    return edge_list


def bucket_index(distance, edge_list):
    bucket_level = jnp.zeros(distance.shape, jnp.int32)
    for edge_value in edge_list:
        bucket_level = bucket_level + (distance >= edge_value).astype(jnp.int32)
    return bucket_level


def attention_kernel(scalars, q_ref, k_ref, v_ref, tc_ref, tn_ref, live_ref, o_ref):
    key_blocks, key_span, head_dim = k_ref.shape
    q_rows = q_ref.shape[0] * q_ref.shape[1]
    cache_rows = tc_ref.shape[2] - q_rows
    new_rows = key_span - cache_rows
    cache_width = tc_ref.shape[2]
    new_width = tn_ref.shape[2]
    query = q_ref[...].reshape(q_rows, head_dim)

    def one_block(g, carry):
        best, weighted, factor_sum = carry
        scores = lax.dot_general(
            query, k_ref[g], (((1,), (1,)), ((), ())), preferred_element_type=jnp.float32
        )
        cache_table = jnp.broadcast_to(tc_ref[0, pl.ds(g, 1), :], (q_rows, cache_width))
        cache_bias = pltpu.roll(cache_table, cache_width - q_rows, 1, stride=1, stride_axis=0)
        new_table = jnp.broadcast_to(tn_ref[0, pl.ds(g, 1), :], (q_rows, new_width))
        new_bias = pltpu.roll(new_table, new_width - q_rows, 1, stride=1, stride_axis=0)
        bias = jnp.concatenate(
            [cache_bias[:, :cache_rows] + live_ref[pl.ds(g, 1), :], new_bias[:, :new_rows]], axis=1
        )
        masked = scores + bias
        peak = jnp.max(masked, axis=1, keepdims=True)
        weights = jnp.exp(masked - peak)
        total = jnp.sum(weights, axis=1, keepdims=True)
        numerator = jnp.dot(
            weights.astype(jnp.bfloat16), v_ref[g], preferred_element_type=jnp.float32
        )
        block_out = (numerator / jnp.maximum(total, 1.0)).astype(jnp.bfloat16).astype(jnp.float32)
        new_best = jnp.maximum(best, peak)
        rescale = jnp.exp(best - new_best)
        factor = jnp.exp(peak - new_best) * total
        return (new_best, weighted * rescale + factor * block_out, factor_sum * rescale + factor)

    start = (
        jnp.full((q_rows, 1), -1e30, jnp.float32),
        jnp.zeros((q_rows, head_dim), jnp.float32),
        jnp.zeros((q_rows, 1), jnp.float32),
    )
    best, weighted, factor_sum = lax.fori_loop(0, key_blocks, one_block, start, unroll=2)
    o_ref[...] = (weighted / factor_sum).astype(o_ref.dtype)


def bias_tables(head_table, length, q_rows, cache_rows, new_rows, query_blocks, key_blocks):
    edges = bucket_edges(head_table.shape[1], MAXDIST)
    blocks = jnp.arange(query_blocks, dtype=jnp.int32)[:, None, None]
    key_ids = jnp.arange(key_blocks, dtype=jnp.int32)[None, :, None]
    cache_lanes = jnp.arange(cache_rows + q_rows, dtype=jnp.int32)[None, None, :]
    new_lanes = jnp.arange(new_rows + q_rows, dtype=jnp.int32)[None, None, :]
    cache_distance = length + blocks * q_rows - key_ids * cache_rows + q_rows - cache_lanes
    new_distance = (blocks * q_rows - key_ids * new_rows) + q_rows - new_lanes
    cache_bucket = bucket_index(jnp.maximum(cache_distance, 0), edges)
    new_bucket = bucket_index(jnp.maximum(new_distance, 0), edges)
    choices = jnp.arange(head_table.shape[1], dtype=jnp.int32)
    cache_hot = (cache_bucket[..., None] == choices).astype(jnp.float32)
    new_hot = (new_bucket[..., None] == choices).astype(jnp.float32)
    cache_table = jnp.einsum("agmk,hk->agm", cache_hot, head_table, precision=lax.Precision.HIGHEST)
    new_table = jnp.einsum("agmk,hk->agm", new_hot, head_table, precision=lax.Precision.HIGHEST)
    new_table = jnp.where(new_distance >= 0, new_table, -1e30)
    cache_slots = key_ids[0] * cache_rows + jnp.arange(cache_rows, dtype=jnp.int32)[None, :]
    live = jnp.where(cache_slots < length, 0.0, -1e30).astype(jnp.float32)
    return cache_table, new_table, live


def block_partials(packed, head_table, length, cache_rows, q_rows):
    source_rows = q_rows
    q_rows = 4 * q_rows
    key_blocks, packed_rows, head_dim = packed.shape
    key_span = (packed_rows - source_rows) // 2
    new_rows = key_span - cache_rows
    query_total = key_blocks * source_rows
    query_blocks = query_total // q_rows
    sources = q_rows // source_rows
    query_offset = 2 * key_span // source_rows
    cache_table, new_table, live = bias_tables(
        head_table, length, q_rows, cache_rows, new_rows, query_blocks, key_blocks
    )
    scalars = jnp.stack([length]).astype(jnp.int32)
    grid_spec = pltpu.PrefetchScalarGridSpec(
        num_scalar_prefetch=1,
        grid=(query_blocks,),
        in_specs=[
            pl.BlockSpec((sources, source_rows, head_dim), lambda b, s: (b, query_offset, 0)),
            pl.BlockSpec((key_blocks, key_span, head_dim), lambda b, s: (0, 0, 0)),
            pl.BlockSpec((key_blocks, key_span, head_dim), lambda b, s: (0, 1, 0)),
            pl.BlockSpec((1, key_blocks, cache_table.shape[2]), lambda b, s: (b, 0, 0)),
            pl.BlockSpec((1, key_blocks, new_table.shape[2]), lambda b, s: (b, 0, 0)),
            pl.BlockSpec(live.shape, lambda b, s: (0, 0)),
        ],
        out_specs=pl.BlockSpec((q_rows, head_dim), lambda b, s: (b, 0)),
    )
    pairs = query_total * key_span * key_blocks
    return pl.pallas_call(
        attention_kernel,
        grid_spec=grid_spec,
        out_shape=jax.ShapeDtypeStruct((query_total, head_dim), jnp.bfloat16),
        cost_estimate=pl.CostEstimate(
            flops=4 * pairs * head_dim,
            transcendentals=pairs,
            bytes_accessed=4 * query_total * head_dim * key_blocks + 4 * key_span * key_blocks * head_dim,
        ),
    )(scalars, packed, packed, packed, cache_table, new_table, live)


def per_device(
    queries,
    new_keys,
    new_values,
    cache_keys,
    cache_values,
    cache_lengths,
    relative_bias,
    residual,
    out_weight,
    norm_gain,
    router_weight,
    routes,
    gate_weight,
    up_weight,
    down_weight,
):
    cut_count = lax.axis_size("cuts")
    cut_index = lax.axis_index("cuts")
    q_rows = queries.shape[1]
    cache_rows = cache_keys.shape[1]
    model_width = queries.shape[2]
    head_count = relative_bias.shape[0]
    head_dim = model_width // head_count
    bucket_count = relative_bias.shape[1]
    length = cache_lengths[0]
    query_total = q_rows * cut_count
    local_keys = jnp.concatenate([cache_keys[0], new_keys[0]], axis=0)
    local_values = jnp.concatenate([cache_values[0], new_values[0]], axis=0)
    key_span = local_keys.shape[0]
    packed = jnp.concatenate(
        [local_keys, local_values, queries[0] * jnp.asarray(0.125, queries.dtype)], axis=0
    )
    packed = lax.all_to_all(
        packed.reshape(packed.shape[0], head_count, head_dim), "cuts", split_axis=1, concat_axis=0, tiled=True
    ).reshape(cut_count, packed.shape[0], head_dim)
    head_table = lax.dynamic_slice_in_dim(relative_bias, cut_index, 1, 0)
    head_out = block_partials(packed, head_table, length, cache_rows, q_rows)
    attended = lax.all_to_all(
        head_out.reshape(cut_count, q_rows, head_dim), "cuts", split_axis=0, concat_axis=0, tiled=True
    ).transpose(1, 0, 2).reshape(q_rows, model_width)
    hidden = residual[0].astype(jnp.float32) + jnp.dot(
        attended, out_weight, preferred_element_type=jnp.float32
    )
    inv_rms = lax.rsqrt(jnp.mean(hidden * hidden, axis=1, keepdims=True) + 1e-06)
    normed = (hidden * inv_rms * norm_gain.astype(jnp.float32)).astype(jnp.bfloat16)
    experts = router_weight.shape[1]
    capacity = (10 * q_rows + 4 * experts - 1) // (4 * experts)
    logits = jnp.dot(normed, router_weight, preferred_element_type=jnp.float32)
    chosen = routes[0]
    onehot = (chosen[:, :, None] == jnp.arange(experts, dtype=jnp.int32)[None, None, :]).astype(
        jnp.float32
    )
    gate_values = jax.nn.sigmoid(jnp.sum(onehot * logits[:, None, :], axis=2))
    named_count = jnp.sum(onehot, axis=1)
    earlier_mask = (jnp.arange(q_rows)[:, None] > jnp.arange(q_rows)[None, :]).astype(jnp.bfloat16)
    earlier = jnp.dot(
        earlier_mask, named_count.astype(jnp.bfloat16), preferred_element_type=jnp.float32
    )
    slot_number = jnp.sum(onehot * earlier[:, None, :], axis=2)
    slot_hot = (
        slot_number[:, :, None] == jnp.arange(capacity, dtype=jnp.float32)[None, None, :]
    ).astype(jnp.float32)
    dispatch = jnp.einsum("tke,tkc->ect", onehot, slot_hot)
    buffers = jnp.einsum(
        "ect,td->ecd", dispatch.astype(jnp.bfloat16), normed, preferred_element_type=jnp.float32
    ).astype(jnp.bfloat16)
    arrived = lax.all_to_all(buffers, "req", split_axis=0, concat_axis=0, tiled=True)
    full_gate = lax.all_gather(gate_weight[0], "cuts", axis=1, tiled=True)
    full_up = lax.all_gather(up_weight[0], "cuts", axis=1, tiled=True)
    full_down = lax.all_gather(down_weight[0], "cuts", axis=1, tiled=True)
    flat_rows = arrived.reshape(-1, model_width)
    gate_act = jnp.dot(flat_rows, full_gate, preferred_element_type=jnp.float32)
    up_act = jnp.dot(flat_rows, full_up, preferred_element_type=jnp.float32)
    act_rows = (jax.nn.gelu(gate_act) * up_act).astype(jnp.bfloat16)
    expert_out = lax.dot_general(
        act_rows, full_down, (((1,), (1,)), ((), ())), preferred_element_type=jnp.float32
    ).astype(jnp.bfloat16).reshape(arrived.shape)
    returned = lax.all_to_all(expert_out, "req", split_axis=0, concat_axis=0, tiled=True)
    combine = jnp.einsum(
        "tke,tkc,tk->ect", onehot, slot_hot, gate_values, precision=lax.Precision.HIGHEST
    )
    gathered_back = jnp.einsum(
        "ect,ecd->td", combine, returned.astype(jnp.float32), precision=lax.Precision.HIGHEST
    )
    layer_out = hidden + gathered_back
    return layer_out.astype(jnp.bfloat16)[None]


def solution(mesh):
    return jax.shard_map(
        per_device,
        mesh=mesh,
        in_specs=(
            P("req", "cuts", None),
            P("req", "cuts", None),
            P("req", "cuts", None),
            P("req", "cuts", None),
            P("req", "cuts", None),
            P("req"),
            P(),
            P("req", "cuts", None),
            P(),
            P(),
            P(),
            P("req", "cuts", None),
            P("req", None, "cuts"),
            P("req", None, "cuts"),
            P("req", None, "cuts"),
        ),
        out_specs=P("req", "cuts", None),
        check_vma=False,
    )
```

```python
from functools import partial

import jax
import jax.numpy as jnp
import numpy as np
from jax import lax
from jax.sharding import PartitionSpec as P
from jax.experimental import pallas as pl
from jax.experimental.pallas import tpu as pltpu

MAXDIST = 128


def shortened(value):
    return jax.tree.map(lambda a: a.astype(jnp.bfloat16) if a.dtype == jnp.float32 else a, value)


def bucket_number(distance, bucket_count, reach_limit):
    exact_count = bucket_count // 2
    if distance < exact_count:
        return distance
    level_value = exact_count + int(
        np.floor(exact_count * np.log(distance / exact_count) / np.log(reach_limit / exact_count))
    )
    return min(bucket_count - 1, level_value)


def bucket_edges(bucket_count, reach_limit):
    edge_list = []
    for target in range(1, bucket_count):
        probe_value = 0
        while bucket_number(probe_value, bucket_count, reach_limit) < target:
            probe_value += 1
        edge_list.append(probe_value)
    return edge_list


def bucket_index(distance, edge_list):
    bucket_level = jnp.zeros(distance.shape, jnp.int32)
    for edge_value in edge_list:
        bucket_level = bucket_level + (distance >= edge_value).astype(jnp.int32)
    return bucket_level


def attention_kernel(scalars, q_ref, k_ref, v_ref, tc_ref, tn_ref, live_ref, o_ref):
    key_blocks, key_span, head_dim = k_ref.shape
    q_rows = q_ref.shape[0] * q_ref.shape[1]
    cache_rows = tc_ref.shape[2] - q_rows
    new_rows = key_span - cache_rows
    cache_width = tc_ref.shape[2]
    new_width = tn_ref.shape[2]
    query = q_ref[...].reshape(q_rows, head_dim)

    def one_block(g, carry):
        best, weighted, factor_sum = carry
        scores = lax.dot_general(
            query, k_ref[g], (((1,), (1,)), ((), ())), preferred_element_type=jnp.float32
        )
        cache_table = jnp.broadcast_to(tc_ref[0, pl.ds(g, 1), :], (q_rows, cache_width))
        cache_bias = pltpu.roll(cache_table, cache_width - q_rows, 1, stride=1, stride_axis=0)
        new_table = jnp.broadcast_to(tn_ref[0, pl.ds(g, 1), :], (q_rows, new_width))
        new_bias = pltpu.roll(new_table, new_width - q_rows, 1, stride=1, stride_axis=0)
        bias = jnp.concatenate(
            [cache_bias[:, :cache_rows] + live_ref[pl.ds(g, 1), :], new_bias[:, :new_rows]], axis=1
        )
        masked = scores + bias
        peak = jnp.max(masked, axis=1, keepdims=True)
        weights = jnp.exp(masked - peak)
        total = jnp.sum(weights, axis=1, keepdims=True)
        numerator = jnp.dot(
            weights.astype(jnp.bfloat16), v_ref[g], preferred_element_type=jnp.float32
        )
        block_out = (numerator / jnp.maximum(total, 1.0)).astype(jnp.bfloat16).astype(jnp.float32)
        new_best = jnp.maximum(best, peak)
        rescale = jnp.exp(best - new_best)
        factor = jnp.exp(peak - new_best) * total
        return (new_best, weighted * rescale + factor * block_out, factor_sum * rescale + factor)

    start = (
        jnp.full((q_rows, 1), -1e30, jnp.float32),
        jnp.zeros((q_rows, head_dim), jnp.float32),
        jnp.zeros((q_rows, 1), jnp.float32),
    )
    best, weighted, factor_sum = lax.fori_loop(0, key_blocks, one_block, start, unroll=4)
    o_ref[...] = (weighted / factor_sum).astype(o_ref.dtype)


def bias_tables(head_table, length, q_rows, cache_rows, new_rows, query_blocks, key_blocks):
    edges = bucket_edges(head_table.shape[1], MAXDIST)
    blocks = jnp.arange(query_blocks, dtype=jnp.int32)[:, None, None]
    key_ids = jnp.arange(key_blocks, dtype=jnp.int32)[None, :, None]
    cache_lanes = jnp.arange(cache_rows + q_rows, dtype=jnp.int32)[None, None, :]
    new_lanes = jnp.arange(new_rows + q_rows, dtype=jnp.int32)[None, None, :]
    cache_distance = length + blocks * q_rows - key_ids * cache_rows + q_rows - cache_lanes
    new_distance = (blocks * q_rows - key_ids * new_rows) + q_rows - new_lanes
    cache_bucket = bucket_index(jnp.maximum(cache_distance, 0), edges)
    new_bucket = bucket_index(jnp.maximum(new_distance, 0), edges)
    choices = jnp.arange(head_table.shape[1], dtype=jnp.int32)
    cache_hot = (cache_bucket[..., None] == choices).astype(jnp.float32)
    new_hot = (new_bucket[..., None] == choices).astype(jnp.float32)
    cache_table = jnp.einsum("agmk,hk->agm", cache_hot, head_table, precision=lax.Precision.HIGHEST)
    new_table = jnp.einsum("agmk,hk->agm", new_hot, head_table, precision=lax.Precision.HIGHEST)
    new_table = jnp.where(new_distance >= 0, new_table, -1e30)
    cache_slots = key_ids[0] * cache_rows + jnp.arange(cache_rows, dtype=jnp.int32)[None, :]
    live = jnp.where(cache_slots < length, 0.0, -1e30).astype(jnp.float32)
    return cache_table, new_table, live


def block_partials(packed, head_table, length, cache_rows, q_rows):
    source_rows = q_rows
    q_rows = 2 * q_rows
    key_blocks, packed_rows, head_dim = packed.shape
    key_span = (packed_rows - source_rows) // 2
    new_rows = key_span - cache_rows
    query_total = key_blocks * source_rows
    query_blocks = query_total // q_rows
    sources = q_rows // source_rows
    query_offset = 2 * key_span // source_rows
    cache_table, new_table, live = bias_tables(
        head_table, length, q_rows, cache_rows, new_rows, query_blocks, key_blocks
    )
    scalars = jnp.stack([length]).astype(jnp.int32)
    grid_spec = pltpu.PrefetchScalarGridSpec(
        num_scalar_prefetch=1,
        grid=(query_blocks,),
        in_specs=[
            pl.BlockSpec((sources, source_rows, head_dim), lambda b, s: (b, query_offset, 0)),
            pl.BlockSpec((key_blocks, key_span, head_dim), lambda b, s: (0, 0, 0)),
            pl.BlockSpec((key_blocks, key_span, head_dim), lambda b, s: (0, 1, 0)),
            pl.BlockSpec((1, key_blocks, cache_table.shape[2]), lambda b, s: (b, 0, 0)),
            pl.BlockSpec((1, key_blocks, new_table.shape[2]), lambda b, s: (b, 0, 0)),
            pl.BlockSpec(live.shape, lambda b, s: (0, 0)),
        ],
        out_specs=pl.BlockSpec((q_rows, head_dim), lambda b, s: (b, 0)),
    )
    pairs = query_total * key_span * key_blocks
    return pl.pallas_call(
        attention_kernel,
        grid_spec=grid_spec,
        out_shape=jax.ShapeDtypeStruct((query_total, head_dim), jnp.bfloat16),
        cost_estimate=pl.CostEstimate(
            flops=4 * pairs * head_dim,
            transcendentals=pairs,
            bytes_accessed=4 * query_total * head_dim * key_blocks + 4 * key_span * key_blocks * head_dim,
        ),
    )(scalars, packed, packed, packed, cache_table, new_table, live)


def per_device(
    queries,
    new_keys,
    new_values,
    cache_keys,
    cache_values,
    cache_lengths,
    relative_bias,
    residual,
    out_weight,
    norm_gain,
    router_weight,
    routes,
    gate_weight,
    up_weight,
    down_weight,
):
    cut_count = lax.axis_size("cuts")
    cut_index = lax.axis_index("cuts")
    q_rows = queries.shape[1]
    cache_rows = cache_keys.shape[1]
    model_width = queries.shape[2]
    head_count = relative_bias.shape[0]
    head_dim = model_width // head_count
    bucket_count = relative_bias.shape[1]
    length = cache_lengths[0]
    query_total = q_rows * cut_count
    local_keys = jnp.concatenate([cache_keys[0], new_keys[0]], axis=0)
    local_values = jnp.concatenate([cache_values[0], new_values[0]], axis=0)
    key_span = local_keys.shape[0]
    packed = jnp.concatenate(
        [local_keys, local_values, queries[0] * jnp.asarray(0.125, queries.dtype)], axis=0
    )
    packed = lax.all_to_all(
        packed.reshape(packed.shape[0], head_count, head_dim), "cuts", split_axis=1, concat_axis=0, tiled=True
    ).reshape(cut_count, packed.shape[0], head_dim)
    head_table = lax.dynamic_slice_in_dim(relative_bias, cut_index, 1, 0)
    head_out = block_partials(packed, head_table, length, cache_rows, q_rows)
    attended = lax.all_to_all(
        head_out.reshape(cut_count, q_rows, head_dim), "cuts", split_axis=0, concat_axis=0, tiled=True
    ).transpose(1, 0, 2).reshape(q_rows, model_width)
    hidden = residual[0].astype(jnp.float32) + jnp.dot(
        attended, out_weight, preferred_element_type=jnp.float32
    )
    inv_rms = lax.rsqrt(jnp.mean(hidden * hidden, axis=1, keepdims=True) + 1e-06)
    normed = (hidden * inv_rms * norm_gain.astype(jnp.float32)).astype(jnp.bfloat16)
    experts = router_weight.shape[1]
    capacity = (10 * q_rows + 4 * experts - 1) // (4 * experts)
    logits = jnp.dot(normed, router_weight, preferred_element_type=jnp.float32)
    chosen = routes[0]
    onehot = (chosen[:, :, None] == jnp.arange(experts, dtype=jnp.int32)[None, None, :]).astype(
        jnp.float32
    )
    gate_values = jax.nn.sigmoid(jnp.sum(onehot * logits[:, None, :], axis=2))
    named_count = jnp.sum(onehot, axis=1)
    earlier_mask = (jnp.arange(q_rows)[:, None] > jnp.arange(q_rows)[None, :]).astype(jnp.bfloat16)
    earlier = jnp.dot(
        earlier_mask, named_count.astype(jnp.bfloat16), preferred_element_type=jnp.float32
    )
    slot_number = jnp.sum(onehot * earlier[:, None, :], axis=2)
    slot_hot = (
        slot_number[:, :, None] == jnp.arange(capacity, dtype=jnp.float32)[None, None, :]
    ).astype(jnp.float32)
    dispatch = jnp.einsum("tke,tkc->ect", onehot, slot_hot)
    buffers = jnp.einsum(
        "ect,td->ecd", dispatch.astype(jnp.bfloat16), normed, preferred_element_type=jnp.float32
    ).astype(jnp.bfloat16)
    arrived = lax.all_to_all(buffers, "req", split_axis=0, concat_axis=0, tiled=True)
    full_gate = lax.all_gather(gate_weight[0], "cuts", axis=1, tiled=True)
    full_up = lax.all_gather(up_weight[0], "cuts", axis=1, tiled=True)
    full_down = lax.all_gather(down_weight[0], "cuts", axis=1, tiled=True)
    flat_rows = arrived.reshape(-1, model_width)
    gate_act = jnp.dot(flat_rows, full_gate, preferred_element_type=jnp.float32)
    up_act = jnp.dot(flat_rows, full_up, preferred_element_type=jnp.float32)
    act_rows = (jax.nn.gelu(gate_act) * up_act).astype(jnp.bfloat16)
    expert_out = lax.dot_general(
        act_rows, full_down, (((1,), (1,)), ((), ())), preferred_element_type=jnp.float32
    ).astype(jnp.bfloat16).reshape(arrived.shape)
    returned = lax.all_to_all(expert_out, "req", split_axis=0, concat_axis=0, tiled=True)
    combine = jnp.einsum(
        "tke,tkc,tk->ect", onehot, slot_hot, gate_values, precision=lax.Precision.HIGHEST
    )
    gathered_back = jnp.einsum(
        "ect,ecd->td", combine, returned.astype(jnp.float32), precision=lax.Precision.HIGHEST
    )
    layer_out = hidden + gathered_back
    return layer_out.astype(jnp.bfloat16)[None]


def solution(mesh):
    return jax.shard_map(
        per_device,
        mesh=mesh,
        in_specs=(
            P("req", "cuts", None),
            P("req", "cuts", None),
            P("req", "cuts", None),
            P("req", "cuts", None),
            P("req", "cuts", None),
            P("req"),
            P(),
            P("req", "cuts", None),
            P(),
            P(),
            P(),
            P("req", "cuts", None),
            P("req", None, "cuts"),
            P("req", None, "cuts"),
            P("req", None, "cuts"),
        ),
        out_specs=P("req", "cuts", None),
        check_vma=False,
    )
```
